32 devices in a mesh: dp: 8 (over z, x), own: 4 (over y, core).
Axes of the slice: x: 2, y: 2, z: 4, core: 2. Of those that a mesh axis runs over, the one named last changes fastest.
Arguments:
- grads_fc: bfloat16 [8, 4, 8, 200, 1600], P('dp', 'own'), may hold values from -180 to 180
- grads_ln: bfloat16 [8, 4, 1600], P('dp'), may hold values from -48 to 48
- grads_emb: bfloat16 [8, 4, 8, 4, 1600], P('dp', 'own'), may hold values from -48 to 48
- weights_fc: bfloat16 [4, 8, 200, 1600], P('own'), may hold values from -0.15625 to 0.15625
- basis: float32 [1600, 256], replicated, may hold values from -0.15625 to 0.15625
- fc_m: float32 [4, 8, 200, 256], P('own', 'dp'), may hold values from -0.6 to 0.6
- fc_v: float32 [4, 8, 200, 256], P('own', 'dp'), may hold values from 0.001 to 0.1
- ln_params: float32 [4, 1600], replicated, may hold values from -3 to 3
- ln_m: float32 [4, 1600], replicated, may hold values from -0.6 to 0.6
- ln_v: float32 [4, 1600], replicated, may hold values from 0.001 to 0.1
- emb_weights: bfloat16 [4, 8, 4, 1600], P('own'), may hold values from -0.29882812 to 0.29882812
- emb_m: float32 [4, 8, 4, 1600], P('own', 'dp'), may hold values from -0.6 to 0.6
- emb_v: float32 [4, 8, 4, 1600], P('own', 'dp'), may hold values from 0.001 to 0.1
- step_count: int32 [1], replicated, may hold values from 1 to 63
Outputs:
- fc_m_next: float32 [4, 8, 200, 256], P('own', 'dp')
- fc_v_next: float32 [4, 8, 200, 256], P('own', 'dp')
- fc_direction: float32 [4, 8, 200, 256], P('own', 'dp')
- weights_next: bfloat16 [4, 8, 200, 1600], P('own')
- basis_next: float32 [1600, 256], replicated
- ln_next: float32 [4, 1600], replicated
- ln_m_next: float32 [4, 1600], replicated
- ln_v_next: float32 [4, 1600], replicated
- emb_next: bfloat16 [4, 8, 4, 1600], P('own')
- emb_m_next: float32 [4, 8, 4, 1600], P('own', 'dp')
- emb_v_next: float32 [4, 8, 4, 1600], P('own', 'dp')
The draws below stay inside these ranges and needn't reach their ends.
All inputs are finite; a program needn't handle non-finite values.
Results may differ from the reference program's by a relative error of at most 0.009.
Values may be sent and summed in bfloat16 or wider, within the bound.
No kernel may reach another device: no remote copies, remote signals or barrier semaphores. Data moves between devices by JAX's collectives and lax.ppermute only.
A program may use at most 128 MiB of HBM per device.

```python
import math
import jax
import jax.numpy as jnp
from jax import lax

D = 1600
FF = 6400
RANK = 256
NS_STEPS = 5
EMB_DEV = 4
FC_ROWS = 200
N_DP = 8
N_OWN = 4


def draw_grads_fc(key, part):
    key_rows, key_base = jax.random.split(key, 2)
    shape = (N_DP, N_OWN, N_DP, FC_ROWS, D)
    position = (jnp.arange(N_OWN)[:, None, None] * N_DP + jnp.arange(N_DP)[None, :, None]) * FC_ROWS + jnp.arange(FC_ROWS)[None, None, :]
    rising = 1.0 + 2.0 * position.astype(jnp.float32) / FF
    rough = jnp.exp(jax.random.uniform(key_rows, (N_OWN, N_DP, FC_ROWS), jnp.float32) * math.log(10.0))
    row_scale = (rising * rough)[None, :, :, :, None]
    base_values = jnp.clip(jax.random.normal(key_base, shape, jnp.float32), -6.0, 6.0)
    return (base_values * row_scale).astype(jnp.bfloat16)


def strengthened(entries, rng, source, target, shards_of, factor):
    def block_of(dim):
        return (jnp.arange(entries.shape[dim]) // (entries.shape[dim] // shards_of)).reshape((-1,) + (1,) * (entries.ndim - 1 - dim))

    first = jax.random.permutation(rng, shards_of)[block_of(target)]
    other_side = (block_of(target) + shards_of // 2) % shards_of
    return jnp.where((block_of(source) == first) | (block_of(source) == other_side), factor * entries, entries)


def shard_levels(stream_key, dims, pieces, least, largest):
    loudness = 1.0
    for dim, blocks in pieces:
        draws = jax.random.uniform(jax.random.fold_in(jax.random.fold_in(stream_key, 6), dim), (blocks,), jnp.float32, least / len(pieces), largest / len(pieces))
        loudness = loudness * jnp.repeat(jnp.exp(draws), dims[dim] // blocks).reshape((-1,) + (1,) * (len(dims) - 1 - dim))
    return loudness


def normal_values(rng, shape, scale, limit, shards=(), held_as=jnp.bfloat16):
    loudness = shard_levels(rng, shape, shards, -0.22, 0.18) if shards else 1.0
    drawn = jax.random.normal(rng, shape, jnp.float32) * scale * loudness
    return jnp.minimum(jnp.maximum(drawn, -limit), limit).astype(held_as)


def gaussian_with(stream_key, extent, scale, bound, pieces, heavy, kind=jnp.bfloat16):
    result = scale * jax.random.normal(stream_key, extent, jnp.float32)
    if pieces:
        result = result * shard_levels(stream_key, extent, pieces, -0.22, 0.18)
    return jnp.clip(strengthened(result, jax.random.fold_in(stream_key, 3), *heavy), -bound, bound).astype(kind)


def setup_inputs(seed: int = 0) -> dict:
    key_of = jax.random.split(jax.random.key(seed), 15)
    grads_fc = draw_grads_fc(jax.random.fold_in(key_of[14], 71), 0)
    grads_ln = normal_values(key_of[1], (N_DP, 4, D), 8.0, 48.0, ((0, 8),))
    grads_emb = gaussian_with(key_of[2], (N_DP, N_OWN, N_DP, EMB_DEV, D), 8.0, 48.0, ((0, 8), (1, 4)), (0, 2, 8, 2.0))
    weights_fc = normal_values(key_of[3], (N_OWN, N_DP, FC_ROWS, D), D ** -0.5, 0.15625, ((0, 4),))
    basis = normal_values(key_of[4], (D, RANK), D ** -0.5, 0.15625, (), jnp.float32)
    fc_m = normal_values(key_of[5], (N_OWN, N_DP, FC_ROWS, RANK), 0.1, 0.6, ((0, 4), (1, 8)), jnp.float32)
    fc_v = jnp.clip(jnp.exp(math.log(0.1) - 4.6051702 * jax.random.uniform(key_of[6], (N_OWN, N_DP, FC_ROWS, RANK), jnp.float32) ** shard_levels(key_of[6], (N_OWN, N_DP, FC_ROWS, RANK), ((0, 4), (1, 8)), -0.2, 0.2)), 0.001, 0.1)
    ln_params = normal_values(key_of[7], (4, D), 0.5, 3.0, (), jnp.float32)
    ln_m = normal_values(key_of[8], (4, D), 0.1, 0.6, (), jnp.float32)
    ln_v = jnp.clip(jnp.exp(jax.random.uniform(key_of[9], (4, D), jnp.float32, math.log(0.001), math.log(0.1))), 0.001, 0.1)
    emb_weights = normal_values(key_of[10], (N_OWN, N_DP, EMB_DEV, D), 0.05, 0.29882812, ((0, 4),))
    emb_m = normal_values(key_of[11], (N_OWN, N_DP, EMB_DEV, D), 0.1, 0.6, ((0, 4), (1, 8)), jnp.float32)
    emb_v = jnp.clip(jnp.exp(math.log(0.1) - 4.6051702 * jax.random.uniform(key_of[12], (N_OWN, N_DP, EMB_DEV, D), jnp.float32) ** shard_levels(key_of[12], (N_OWN, N_DP, EMB_DEV, D), ((0, 4), (1, 8)), -0.2, 0.2)), 0.001, 0.1)
    step_count = jax.random.randint(key_of[13], (1,), 1, 64).astype(jnp.int32)
    return {"grads_fc": grads_fc, "grads_ln": grads_ln, "grads_emb": grads_emb, "weights_fc": weights_fc, "basis": basis, "fc_m": fc_m, "fc_v": fc_v, "ln_params": ln_params, "ln_m": ln_m, "ln_v": ln_v, "emb_weights": emb_weights, "emb_m": emb_m, "emb_v": emb_v, "step_count": step_count}


beta_one = 0.9
beta_two = 0.999
adam_eps = 1e-08
learn_rate = 0.02
galore_scale = 0.25

def adam_update(moment_one, moment_two, gradient, correct_one, correct_two):
    moment_one_new = beta_one * moment_one + (1.0 - beta_one) * gradient
    moment_two_new = beta_two * moment_two + (1.0 - beta_two) * gradient * gradient
    direction = moment_one_new / correct_one / (jnp.sqrt(moment_two_new / correct_two) + adam_eps)
    return (moment_one_new, moment_two_new, direction)

def orthogonalize(subspace):
    highest = lax.Precision.HIGHEST
    iterate = subspace * lax.rsqrt(jnp.sum(subspace * subspace) + 1e-06)
    for sweep_index in range(NS_STEPS):
        gram_matrix = jnp.dot(iterate.T, iterate, precision=highest)
        iterate = 1.5 * iterate - 0.5 * jnp.dot(iterate, gram_matrix, precision=highest)
    return iterate

def reference(grads_fc, grads_ln, grads_emb, weights_fc, basis, fc_m, fc_v, ln_params, ln_m, ln_v, emb_weights, emb_m, emb_v, step_count):
    highest = lax.Precision.HIGHEST
    grad_sum = lax.optimization_barrier(jnp.sum(grads_fc, axis=0, dtype=jnp.float32)).reshape(FF, D)
    emb_sum = lax.optimization_barrier(jnp.sum(grads_emb, axis=0, dtype=jnp.float32))
    ln_sum = lax.optimization_barrier(jnp.sum(grads_ln, axis=0, dtype=jnp.float32))
    projected = jnp.dot(grad_sum, basis, precision=highest)
    subspace = jnp.dot(grad_sum.T, projected, precision=highest)
    squares = jnp.sum(projected * projected) + jnp.sum(emb_sum * emb_sum) + jnp.sum(ln_sum * ln_sum)
    grad_norm = jnp.sqrt(squares + 1e-06)
    clip_limit = math.sqrt(FF * RANK + EMB_DEV * N_DP * N_OWN * D + 4 * D)
    factor = jnp.minimum(1.0, clip_limit / grad_norm)
    count = step_count[0].astype(jnp.float32)
    correct_one = 1.0 - jnp.power(jnp.float32(beta_one), count)
    correct_two = 1.0 - jnp.power(jnp.float32(beta_two), count)
    fc_grad = factor * projected.reshape(N_OWN, N_DP, FC_ROWS, RANK)
    fc_m_next, fc_v_next, fc_direction = adam_update(fc_m, fc_v, fc_grad, correct_one, correct_two)
    update = jnp.dot(fc_direction.reshape(FF, RANK), basis.T, precision=highest).reshape(N_OWN, N_DP, FC_ROWS, D)
    weights_next = (weights_fc.astype(jnp.float32) - learn_rate * galore_scale * update).astype(jnp.bfloat16)
    ln_m_next, ln_v_next, ln_direction = adam_update(ln_m, ln_v, factor * ln_sum, correct_one, correct_two)
    ln_next = ln_params - learn_rate * ln_direction
    emb_m_next, emb_v_next, emb_direction = adam_update(emb_m, emb_v, factor * emb_sum, correct_one, correct_two)
    emb_next = (emb_weights.astype(jnp.float32) - learn_rate * emb_direction).astype(jnp.bfloat16)
    basis_next = orthogonalize(subspace)
    return (fc_m_next, fc_v_next, fc_direction, weights_next, basis_next, ln_next, ln_m_next, ln_v_next, emb_next, emb_m_next, emb_v_next)
```

```python
import math

import jax
import jax.numpy as jnp
from jax import lax
from jax.sharding import PartitionSpec as P

FF = 6400
RANK = 256
NS_STEPS = 5


beta_one = 0.9
beta_two = 0.999
adam_eps = 1e-08
learn_rate = 0.02
galore_scale = 0.25


def adam_update(moment_one, moment_two, gradient, correct_one, correct_two):
    moment_one_new = beta_one * moment_one + (1.0 - beta_one) * gradient
    moment_two_new = beta_two * moment_two + (1.0 - beta_two) * gradient * gradient
    direction = moment_one_new / correct_one / (jnp.sqrt(moment_two_new / correct_two) + adam_eps)
    return (moment_one_new, moment_two_new, direction)


def orthogonalize(subspace):
    highest = lax.Precision.HIGHEST
    iterate = subspace * lax.rsqrt(jnp.sum(subspace * subspace) + 1e-06)
    for sweep_index in range(NS_STEPS):
        gram_matrix = jnp.dot(iterate.T, iterate, precision=highest)
        iterate = 1.5 * iterate - 0.5 * jnp.dot(iterate, gram_matrix, precision=highest)
    return iterate


def row_count_of(piece, cols):
    return -(-piece.size // cols)


def pack_rows(pieces, cols):
    rows = []
    for piece in pieces:
        if piece.ndim == 2 and piece.shape[1] == cols:
            rows.append(piece)
            continue
        flat = piece.reshape(-1)
        flat = jnp.pad(flat, (0, row_count_of(piece, cols) * cols - flat.size))
        rows.append(flat.reshape(-1, cols))
    return jnp.concatenate(rows, axis=0)


def unpack_rows(packed, pieces):
    cols = packed.shape[1]
    out = []
    start = 0
    for piece in pieces:
        count = row_count_of(piece, cols)
        block = packed[start : start + count]
        start += count
        out.append(block.reshape(-1)[: piece.size].reshape(piece.shape))
    return out


def split3(values):
    first = values.astype(jnp.bfloat16)
    rest = values - first.astype(jnp.float32)
    second = rest.astype(jnp.bfloat16)
    third = (rest - second.astype(jnp.float32)).astype(jnp.bfloat16)
    return jnp.concatenate([first, second, third], axis=1)


def exact_dot(lhs_bf16, rhs_f32, contract):
    cols = rhs_f32.shape[1]
    wide = lax.dot_general(
        lhs_bf16,
        split3(rhs_f32),
        ((contract, (0,)), ((), ())),
        preferred_element_type=jnp.float32,
    )
    return wide[:, :cols] + wide[:, cols : 2 * cols] + wide[:, 2 * cols :]


def shards(
    grads_fc,
    grads_ln,
    grads_emb,
    weights_fc,
    basis,
    fc_m,
    fc_v,
    ln_params,
    ln_m,
    ln_v,
    emb_weights,
    emb_m,
    emb_v,
    step_count,
):
    highest = lax.Precision.HIGHEST
    replicas = lax.axis_size("dp")
    owners = lax.axis_size("own")
    replica = lax.axis_index("dp")
    blocks = grads_fc.shape[2]
    row_count = grads_fc.shape[3]
    width = grads_fc.shape[4]
    rank_cols = basis.shape[1]
    emb_count = grads_emb.shape[3]
    local_rows = grads_fc.reshape(blocks * row_count, width)
    local_proj = exact_dot(local_rows, basis, (1,))
    emb_local = grads_emb.reshape(blocks, emb_count, width).astype(jnp.float32)
    ln_local = grads_ln.reshape(4, width).astype(jnp.float32)
    proj_own, emb_own, ln_sum = unpack_rows(
        lax.psum(pack_rows((local_proj, emb_local, ln_local), rank_cols), "dp"),
        (local_proj, emb_local, ln_local),
    )
    partial_value = exact_dot(local_rows, proj_own, (0,))
    own_square = jnp.sum(proj_own * proj_own) + jnp.sum(emb_own * emb_own)
    own_square = jnp.where(replica == 0, own_square, 0.0)
    subspace, square_total = unpack_rows(
        lax.psum(pack_rows((partial_value, own_square), rank_cols), ("dp", "own")),
        (partial_value, own_square),
    )
    grad_norm = jnp.sqrt(square_total + jnp.sum(ln_sum * ln_sum) + 1e-06)
    clip_limit = math.sqrt(FF * RANK + emb_count * replicas * owners * width + 4 * width)
    factor = jnp.minimum(1.0, clip_limit / grad_norm)
    count = step_count[0].astype(jnp.float32)
    correct_one = 1.0 - jnp.power(jnp.float32(beta_one), count)
    correct_two = 1.0 - jnp.power(jnp.float32(beta_two), count)
    proj_rows = lax.dynamic_slice_in_dim(proj_own, replica * row_count, row_count, 0)
    fc_grad = factor * proj_rows.reshape(1, 1, row_count, rank_cols)
    fc_m_next, fc_v_next, fc_direction = adam_update(fc_m, fc_v, fc_grad, correct_one, correct_two)
    ln_m_next, ln_v_next, ln_direction = adam_update(
        ln_m, ln_v, factor * ln_sum, correct_one, correct_two
    )
    ln_next = ln_params - learn_rate * ln_direction
    emb_rows = lax.dynamic_index_in_dim(emb_own, replica, 0, keepdims=True).reshape(
        1, 1, emb_count, width
    )
    emb_m_next, emb_v_next, emb_direction = adam_update(
        emb_m, emb_v, factor * emb_rows, correct_one, correct_two
    )
    fc_dir_mine = fc_direction.reshape(row_count, rank_cols)
    emb_dir_mine = emb_direction.reshape(emb_count, width)
    gathered = lax.all_gather(
        pack_rows((fc_dir_mine, emb_dir_mine), rank_cols), "dp", axis=0, tiled=False
    )
    fc_dir_all, emb_dir_all = jax.vmap(
        lambda packed: unpack_rows(packed, (fc_dir_mine, emb_dir_mine))
    )(gathered)
    fc_dir_all = fc_dir_all.reshape(replicas * row_count, rank_cols)
    update_rows = jnp.dot(fc_dir_all, basis.T, precision=highest)
    weights_next = (
        weights_fc.astype(jnp.float32)
        - learn_rate * galore_scale * update_rows.reshape(weights_fc.shape)
    ).astype(jnp.bfloat16)
    emb_next = (
        emb_weights.astype(jnp.float32) - learn_rate * emb_dir_all.reshape(emb_weights.shape)
    ).astype(jnp.bfloat16)
    basis_next = orthogonalize(subspace)
    return (
        fc_m_next,
        fc_v_next,
        fc_direction,
        weights_next,
        basis_next,
        ln_next,
        ln_m_next,
        ln_v_next,
        emb_next,
        emb_m_next,
        emb_v_next,
    )


def solution(mesh):
    in_specs = (
        P("dp", "own", None, None, None),
        P("dp", None, None),
        P("dp", "own", None, None, None),
        P("own", None, None, None),
        P(),
        P("own", "dp", None, None),
        P("own", "dp", None, None),
        P(),
        P(),
        P(),
        P("own", None, None, None),
        P("own", "dp", None, None),
        P("own", "dp", None, None),
        P(),
    )
    out_specs = (
        P("own", "dp", None, None),
        P("own", "dp", None, None),
        P("own", "dp", None, None),
        P("own", None, None, None),
        P(),
        P(),
        P(),
        P(),
        P("own", None, None, None),
        P("own", "dp", None, None),
        P("own", "dp", None, None),
    )
    return jax.shard_map(shards, mesh=mesh, in_specs=in_specs, out_specs=out_specs, check_vma=False)
```

```python
import math

import jax
import jax.numpy as jnp
from jax import lax
from jax.sharding import PartitionSpec as P

FF = 6400
RANK = 256
NS_STEPS = 5


beta_one = 0.9
beta_two = 0.999
adam_eps = 1e-08
learn_rate = 0.02
galore_scale = 0.25


def adam_update(moment_one, moment_two, gradient, correct_one, correct_two):
    moment_one_new = beta_one * moment_one + (1.0 - beta_one) * gradient
    moment_two_new = beta_two * moment_two + (1.0 - beta_two) * gradient * gradient
    direction = moment_one_new / correct_one / (jnp.sqrt(moment_two_new / correct_two) + adam_eps)
    return (moment_one_new, moment_two_new, direction)


def orthogonalize(subspace):
    highest = lax.Precision.HIGHEST
    iterate = subspace * lax.rsqrt(jnp.sum(subspace * subspace) + 1e-06)
    for sweep_index in range(NS_STEPS):
        gram_matrix = jnp.dot(iterate.T, iterate, precision=highest)
        iterate = 1.5 * iterate - 0.5 * jnp.dot(iterate, gram_matrix, precision=highest)
    return iterate


def row_count_of(piece, cols):
    return -(-piece.size // cols)


def pack_rows(pieces, cols):
    rows = []
    for piece in pieces:
        if piece.ndim == 2 and piece.shape[1] == cols:
            rows.append(piece)
            continue
        flat = piece.reshape(-1)
        flat = jnp.pad(flat, (0, row_count_of(piece, cols) * cols - flat.size))
        rows.append(flat.reshape(-1, cols))
    return jnp.concatenate(rows, axis=0)


def unpack_rows(packed, pieces):
    cols = packed.shape[1]
    out = []
    start = 0
    for piece in pieces:
        count = row_count_of(piece, cols)
        block = packed[start : start + count]
        start += count
        out.append(block.reshape(-1)[: piece.size].reshape(piece.shape))
    return out


def axis_steps(axes):
    steps = []
    for name in axes:
        size = lax.axis_size(name)
        if size & (size - 1):
            return None
        bit = 1
        while bit < size:
            steps.append((name, bit, size))
            bit *= 2
    return steps


def swap_with(values, name, bit, size):
    return lax.ppermute(values, name, [(index, index ^ bit) for index in range(size)])


def butterfly_sum(packed, axes):
    steps = axis_steps(axes)
    if steps is None:
        return lax.psum(packed, axes)
    count = 2 ** len(steps)
    rows = packed.shape[0]
    padded = -(-rows // (8 * count)) * 8 * count
    parts = jnp.pad(packed, ((0, padded - rows), (0, 0)))
    sides = []
    for name, bit, size in steps:
        side = (lax.axis_index(name) // bit) % 2
        half = parts.shape[0] // 2
        keep = lax.dynamic_slice_in_dim(parts, side * half, half, 0)
        send = lax.dynamic_slice_in_dim(parts, (1 - side) * half, half, 0)
        parts = keep + swap_with(send, name, bit, size)
        sides.append(side)
    for (name, bit, size), side in zip(reversed(steps), reversed(sides)):
        other = swap_with(parts, name, bit, size)
        first = jnp.where(side == 0, parts, other)
        second = jnp.where(side == 0, other, parts)
        parts = jnp.concatenate([first, second], axis=0)
    return parts[:rows]


def butterfly_gather(piece, name):
    size = lax.axis_size(name)
    if size & (size - 1):
        return lax.all_gather(piece, name, axis=0, tiled=False)
    parts = piece[None]
    bit = 1
    while bit < size:
        side = (lax.axis_index(name) // bit) % 2
        other = swap_with(parts, name, bit, size)
        first = jnp.where(side == 0, parts, other)
        second = jnp.where(side == 0, other, parts)
        parts = jnp.concatenate([first, second], axis=0)
        bit *= 2
    return parts


def split3(values):
    first = values.astype(jnp.bfloat16)
    rest = values - first.astype(jnp.float32)
    second = rest.astype(jnp.bfloat16)
    third = (rest - second.astype(jnp.float32)).astype(jnp.bfloat16)
    return jnp.concatenate([first, second, third], axis=1)


def exact_dot(lhs_bf16, rhs_f32, contract):
    cols = rhs_f32.shape[1]
    wide = lax.dot_general(
        lhs_bf16,
        split3(rhs_f32),
        ((contract, (0,)), ((), ())),
        preferred_element_type=jnp.float32,
    )
    return wide[:, :cols] + wide[:, cols : 2 * cols] + wide[:, 2 * cols :]


def shards(
    grads_fc,
    grads_ln,
    grads_emb,
    weights_fc,
    basis,
    fc_m,
    fc_v,
    ln_params,
    ln_m,
    ln_v,
    emb_weights,
    emb_m,
    emb_v,
    step_count,
):
    highest = lax.Precision.HIGHEST
    replicas = lax.axis_size("dp")
    owners = lax.axis_size("own")
    replica = lax.axis_index("dp")
    blocks = grads_fc.shape[2]
    row_count = grads_fc.shape[3]
    width = grads_fc.shape[4]
    rank_cols = basis.shape[1]
    emb_count = grads_emb.shape[3]
    local_rows = grads_fc.reshape(blocks * row_count, width)
    local_proj = exact_dot(local_rows, basis, (1,))
    emb_local = grads_emb.reshape(blocks, emb_count, width).astype(jnp.float32)
    ln_local = grads_ln.reshape(4, width).astype(jnp.float32)
    proj_own, emb_own, ln_sum = unpack_rows(
        butterfly_sum(pack_rows((local_proj, emb_local, ln_local), rank_cols), ("dp",)),
        (local_proj, emb_local, ln_local),
    )
    partial_value = exact_dot(local_rows, proj_own, (0,))
    own_square = jnp.sum(proj_own * proj_own) + jnp.sum(emb_own * emb_own)
    own_square = jnp.where(replica == 0, own_square, 0.0)
    subspace, square_total = unpack_rows(
        butterfly_sum(pack_rows((partial_value, own_square), rank_cols), ("own", "dp")),
        (partial_value, own_square),
    )
    grad_norm = jnp.sqrt(square_total + jnp.sum(ln_sum * ln_sum) + 1e-06)
    clip_limit = math.sqrt(FF * RANK + emb_count * replicas * owners * width + 4 * width)
    factor = jnp.minimum(1.0, clip_limit / grad_norm)
    count = step_count[0].astype(jnp.float32)
    correct_one = 1.0 - jnp.power(jnp.float32(beta_one), count)
    correct_two = 1.0 - jnp.power(jnp.float32(beta_two), count)
    proj_rows = lax.dynamic_slice_in_dim(proj_own, replica * row_count, row_count, 0)
    fc_grad = factor * proj_rows.reshape(1, 1, row_count, rank_cols)
    fc_m_next, fc_v_next, fc_direction = adam_update(fc_m, fc_v, fc_grad, correct_one, correct_two)
    ln_m_next, ln_v_next, ln_direction = adam_update(
        ln_m, ln_v, factor * ln_sum, correct_one, correct_two
    )
    ln_next = ln_params - learn_rate * ln_direction
    emb_rows = lax.dynamic_index_in_dim(emb_own, replica, 0, keepdims=True).reshape(
        1, 1, emb_count, width
    )
    emb_m_next, emb_v_next, emb_direction = adam_update(
        emb_m, emb_v, factor * emb_rows, correct_one, correct_two
    )
    fc_dir_mine = fc_direction.reshape(row_count, rank_cols)
    emb_dir_mine = emb_direction.reshape(emb_count, width)
    gathered = butterfly_gather(pack_rows((fc_dir_mine, emb_dir_mine), rank_cols), "dp")
    fc_dir_all, emb_dir_all = jax.vmap(
        lambda packed: unpack_rows(packed, (fc_dir_mine, emb_dir_mine))
    )(gathered)
    fc_dir_all = fc_dir_all.reshape(replicas * row_count, rank_cols)
    update_rows = jnp.dot(fc_dir_all, basis.T, precision=highest)
    weights_next = (
        weights_fc.astype(jnp.float32)
        - learn_rate * galore_scale * update_rows.reshape(weights_fc.shape)
    ).astype(jnp.bfloat16)
    emb_next = (
        emb_weights.astype(jnp.float32) - learn_rate * emb_dir_all.reshape(emb_weights.shape)
    ).astype(jnp.bfloat16)
    basis_next = orthogonalize(subspace)
    return (
        fc_m_next,
        fc_v_next,
        fc_direction,
        weights_next,
        basis_next,
        ln_next,
        ln_m_next,
        ln_v_next,
        emb_next,
        emb_m_next,
        emb_v_next,
    )


def solution(mesh):
    in_specs = (
        P("dp", "own", None, None, None),
        P("dp", None, None),
        P("dp", "own", None, None, None),
        P("own", None, None, None),
        P(),
        P("own", "dp", None, None),
        P("own", "dp", None, None),
        P(),
        P(),
        P(),
        P("own", None, None, None),
        P("own", "dp", None, None),
        P("own", "dp", None, None),
        P(),
    )
    out_specs = (
        P("own", "dp", None, None),
        P("own", "dp", None, None),
        P("own", "dp", None, None),
        P("own", None, None, None),
        P(),
        P(),
        P(),
        P(),
        P("own", None, None, None),
        P("own", "dp", None, None),
        P("own", "dp", None, None),
    )
    return jax.shard_map(shards, mesh=mesh, in_specs=in_specs, out_specs=out_specs, check_vma=False)
```

```python
import math

import jax
import jax.numpy as jnp
from jax import lax
from jax.sharding import PartitionSpec as P

FF = 6400
RANK = 256
NS_STEPS = 5


beta_one = 0.9
beta_two = 0.999
adam_eps = 1e-08
learn_rate = 0.02
galore_scale = 0.25


def adam_update(moment_one, moment_two, gradient, correct_one, correct_two):
    moment_one_new = beta_one * moment_one + (1.0 - beta_one) * gradient
    moment_two_new = beta_two * moment_two + (1.0 - beta_two) * gradient * gradient
    direction = moment_one_new / correct_one / (jnp.sqrt(moment_two_new / correct_two) + adam_eps)
    return (moment_one_new, moment_two_new, direction)


def orthogonalize(subspace):
    highest = lax.Precision.HIGHEST
    iterate = subspace * lax.rsqrt(jnp.sum(subspace * subspace) + 1e-06)
    for sweep_index in range(NS_STEPS):
        gram_matrix = jnp.dot(iterate.T, iterate, precision=highest)
        iterate = 1.5 * iterate - 0.5 * jnp.dot(iterate, gram_matrix, precision=highest)
    return iterate


def row_count_of(piece, cols):
    return -(-piece.size // cols)


def pack_rows(pieces, cols):
    rows = []
    for piece in pieces:
        if piece.ndim == 2 and piece.shape[1] == cols:
            rows.append(piece)
            continue
        flat = piece.reshape(-1)
        flat = jnp.pad(flat, (0, row_count_of(piece, cols) * cols - flat.size))
        rows.append(flat.reshape(-1, cols))
    return jnp.concatenate(rows, axis=0)


def unpack_rows(packed, pieces):
    cols = packed.shape[1]
    out = []
    start = 0
    for piece in pieces:
        count = row_count_of(piece, cols)
        block = packed[start : start + count]
        start += count
        out.append(block.reshape(-1)[: piece.size].reshape(piece.shape))
    return out


def axis_steps(axes):
    steps = []
    for name in axes:
        size = lax.axis_size(name)
        if size & (size - 1):
            return None
        bit = 1
        while bit < size:
            steps.append((name, bit, size))
            bit *= 2
    return steps


def swap_with(values, name, bit, size):
    return lax.ppermute(values, name, [(index, index ^ bit) for index in range(size)])


def run_steps(parts, steps):
    sides = []
    for name, bit, size in steps:
        side = (lax.axis_index(name) // bit) % 2
        half = parts.shape[0] // 2
        keep = lax.dynamic_slice_in_dim(parts, side * half, half, 0)
        send = lax.dynamic_slice_in_dim(parts, (1 - side) * half, half, 0)
        parts = keep + swap_with(send, name, bit, size)
        sides.append(side)
    for (name, bit, size), side in zip(reversed(steps), reversed(sides)):
        other = swap_with(parts, name, bit, size)
        first = jnp.where(side == 0, parts, other)
        second = jnp.where(side == 0, other, parts)
        parts = jnp.concatenate([first, second], axis=0)
    return parts


def butterfly_sum(packed, axes):
    steps = axis_steps(axes)
    if steps is None:
        return lax.psum(packed, axes)
    count = 2 ** len(steps)
    rows, cols = packed.shape
    padded = -(-rows // (8 * count)) * 8 * count
    parts = jnp.pad(packed, ((0, padded - rows), (0, 0)))
    low = 1 if len(axes) > 1 else 0
    high = len(steps) - 1
    if cols % 256 or high - low < 2:
        return run_steps(parts, steps)[:rows]
    middle = steps[low:high]
    other = steps[:low] + middle[1:] + middle[:1] + steps[high:]
    half = cols // 2
    left = run_steps(parts[:, :half], steps)
    right = run_steps(parts[:, half:], other)
    return jnp.concatenate([left, right], axis=1)[:rows]


def butterfly_gather(piece, name):
    size = lax.axis_size(name)
    if size & (size - 1):
        return lax.all_gather(piece, name, axis=0, tiled=False)
    parts = piece[None]
    bit = size // 2
    levels = 0
    while bit >= 1:
        side = (lax.axis_index(name) // bit) % 2
        other = swap_with(parts, name, bit, size)
        first = jnp.where(side == 0, parts, other)
        second = jnp.where(side == 0, other, parts)
        parts = jnp.concatenate([first, second], axis=0)
        bit //= 2
        levels += 1
    parts = parts.reshape((2,) * levels + piece.shape)
    order = tuple(reversed(range(levels))) + tuple(range(levels, levels + piece.ndim))
    return parts.transpose(order).reshape((size,) + piece.shape)


def split3(values):
    first = values.astype(jnp.bfloat16)
    rest = values - first.astype(jnp.float32)
    second = rest.astype(jnp.bfloat16)
    third = (rest - second.astype(jnp.float32)).astype(jnp.bfloat16)
    return jnp.concatenate([first, second, third], axis=1)


def exact_dot(lhs_bf16, rhs_f32, contract):
    cols = rhs_f32.shape[1]
    wide = lax.dot_general(
        lhs_bf16,
        split3(rhs_f32),
        ((contract, (0,)), ((), ())),
        preferred_element_type=jnp.float32,
    )
    return wide[:, :cols] + wide[:, cols : 2 * cols] + wide[:, 2 * cols :]


def shards(
    grads_fc,
    grads_ln,
    grads_emb,
    weights_fc,
    basis,
    fc_m,
    fc_v,
    ln_params,
    ln_m,
    ln_v,
    emb_weights,
    emb_m,
    emb_v,
    step_count,
):
    highest = lax.Precision.HIGHEST
    replicas = lax.axis_size("dp")
    owners = lax.axis_size("own")
    replica = lax.axis_index("dp")
    blocks = grads_fc.shape[2]
    row_count = grads_fc.shape[3]
    width = grads_fc.shape[4]
    rank_cols = basis.shape[1]
    emb_count = grads_emb.shape[3]
    local_rows = grads_fc.reshape(blocks * row_count, width)
    local_proj = exact_dot(local_rows, basis, (1,))
    emb_local = grads_emb.reshape(blocks, emb_count, width).astype(jnp.float32)
    ln_local = grads_ln.reshape(4, width).astype(jnp.float32)
    proj_own, emb_own, ln_sum = unpack_rows(
        butterfly_sum(pack_rows((local_proj, emb_local, ln_local), rank_cols), ("dp",)),
        (local_proj, emb_local, ln_local),
    )
    partial_value = exact_dot(local_rows, proj_own, (0,))
    own_square = jnp.sum(proj_own * proj_own) + jnp.sum(emb_own * emb_own)
    own_square = jnp.where(replica == 0, own_square, 0.0)
    subspace, square_total = unpack_rows(
        butterfly_sum(pack_rows((partial_value, own_square), rank_cols), ("own", "dp")),
        (partial_value, own_square),
    )
    grad_norm = jnp.sqrt(square_total + jnp.sum(ln_sum * ln_sum) + 1e-06)
    clip_limit = math.sqrt(FF * RANK + emb_count * replicas * owners * width + 4 * width)
    factor = jnp.minimum(1.0, clip_limit / grad_norm)
    count = step_count[0].astype(jnp.float32)
    correct_one = 1.0 - jnp.power(jnp.float32(beta_one), count)
    correct_two = 1.0 - jnp.power(jnp.float32(beta_two), count)
    proj_rows = lax.dynamic_slice_in_dim(proj_own, replica * row_count, row_count, 0)
    fc_grad = factor * proj_rows.reshape(1, 1, row_count, rank_cols)
    fc_m_next, fc_v_next, fc_direction = adam_update(fc_m, fc_v, fc_grad, correct_one, correct_two)
    ln_m_next, ln_v_next, ln_direction = adam_update(
        ln_m, ln_v, factor * ln_sum, correct_one, correct_two
    )
    ln_next = ln_params - learn_rate * ln_direction
    emb_rows = lax.dynamic_index_in_dim(emb_own, replica, 0, keepdims=True).reshape(
        1, 1, emb_count, width
    )
    emb_m_next, emb_v_next, emb_direction = adam_update(
        emb_m, emb_v, factor * emb_rows, correct_one, correct_two
    )
    fc_dir_mine = fc_direction.reshape(row_count, rank_cols).astype(jnp.bfloat16)
    emb_dir_f32 = emb_direction.reshape(emb_count, width)
    emb_dir_high = emb_dir_f32.astype(jnp.bfloat16)
    emb_dir_low = (emb_dir_f32 - emb_dir_high.astype(jnp.float32)).astype(jnp.bfloat16)
    emb_dir_mine = jnp.stack([emb_dir_high, emb_dir_low])
    gathered = butterfly_gather(pack_rows((fc_dir_mine, emb_dir_mine), rank_cols), "dp")
    fc_dir_all, emb_dir_all = jax.vmap(
        lambda packed: unpack_rows(packed, (fc_dir_mine, emb_dir_mine))
    )(gathered)
    fc_dir_all = fc_dir_all.reshape(replicas * row_count, rank_cols).astype(jnp.float32)
    emb_dir_all = emb_dir_all[:, 0].astype(jnp.float32) + emb_dir_all[:, 1].astype(jnp.float32)
    update_rows = jnp.dot(fc_dir_all, basis.T, precision=highest)
    weights_next = (
        weights_fc.astype(jnp.float32)
        - learn_rate * galore_scale * update_rows.reshape(weights_fc.shape)
    ).astype(jnp.bfloat16)
    emb_next = (
        emb_weights.astype(jnp.float32) - learn_rate * emb_dir_all.reshape(emb_weights.shape)
    ).astype(jnp.bfloat16)
    basis_next = orthogonalize(subspace)
    return (
        fc_m_next,
        fc_v_next,
        fc_direction,
        weights_next,
        basis_next,
        ln_next,
        ln_m_next,
        ln_v_next,
        emb_next,
        emb_m_next,
        emb_v_next,
    )


def solution(mesh):
    in_specs = (
        P("dp", "own", None, None, None),
        P("dp", None, None),
        P("dp", "own", None, None, None),
        P("own", None, None, None),
        P(),
        P("own", "dp", None, None),
        P("own", "dp", None, None),
        P(),
        P(),
        P(),
        P("own", None, None, None),
        P("own", "dp", None, None),
        P("own", "dp", None, None),
        P(),
    )
    out_specs = (
        P("own", "dp", None, None),
        P("own", "dp", None, None),
        P("own", "dp", None, None),
        P("own", None, None, None),
        P(),
        P(),
        P(),
        P(),
        P("own", None, None, None),
        P("own", "dp", None, None),
        P("own", "dp", None, None),
    )
    return jax.shard_map(shards, mesh=mesh, in_specs=in_specs, out_specs=out_specs, check_vma=False)
```

```python
import math

import jax
import jax.numpy as jnp
from jax import lax
from jax.sharding import PartitionSpec as P

FF = 6400
RANK = 256
NS_STEPS = 5


beta_one = 0.9
beta_two = 0.999
adam_eps = 1e-08
learn_rate = 0.02
galore_scale = 0.25


def adam_update(moment_one, moment_two, gradient, correct_one, correct_two):
    moment_one_new = beta_one * moment_one + (1.0 - beta_one) * gradient
    moment_two_new = beta_two * moment_two + (1.0 - beta_two) * gradient * gradient
    direction = moment_one_new / correct_one / (jnp.sqrt(moment_two_new / correct_two) + adam_eps)
    return (moment_one_new, moment_two_new, direction)


def orthogonalize(subspace):
    highest = lax.Precision.HIGH
    iterate = subspace * lax.rsqrt(jnp.sum(subspace * subspace) + 1e-06)
    for sweep_index in range(NS_STEPS):
        gram_matrix = jnp.dot(iterate.T, iterate, precision=highest)
        iterate = 1.5 * iterate - 0.5 * jnp.dot(iterate, gram_matrix, precision=highest)
    return iterate


def row_count_of(piece, cols):
    return -(-piece.size // cols)


def pack_rows(pieces, cols):
    rows = []
    for piece in pieces:
        if piece.ndim == 2 and piece.shape[1] == cols:
            rows.append(piece)
            continue
        flat = piece.reshape(-1)
        flat = jnp.pad(flat, (0, row_count_of(piece, cols) * cols - flat.size))
        rows.append(flat.reshape(-1, cols))
    return jnp.concatenate(rows, axis=0)


def unpack_rows(packed, pieces):
    cols = packed.shape[1]
    out = []
    start = 0
    for piece in pieces:
        count = row_count_of(piece, cols)
        block = packed[start : start + count]
        start += count
        out.append(block.reshape(-1)[: piece.size].reshape(piece.shape))
    return out


def axis_steps(axes):
    steps = []
    for name in axes:
        size = lax.axis_size(name)
        if size & (size - 1):
            return None
        bit = 1
        while bit < size:
            steps.append((name, bit, size))
            bit *= 2
    return steps


def swap_with(values, name, bit, size):
    return lax.ppermute(values, name, [(index, index ^ bit) for index in range(size)])


def run_steps(parts, steps):
    sides = []
    for name, bit, size in steps:
        side = (lax.axis_index(name) // bit) % 2
        half = parts.shape[0] // 2
        keep = lax.dynamic_slice_in_dim(parts, side * half, half, 0)
        send = lax.dynamic_slice_in_dim(parts, (1 - side) * half, half, 0)
        parts = keep + swap_with(send, name, bit, size)
        sides.append(side)
    for (name, bit, size), side in zip(reversed(steps), reversed(sides)):
        other = swap_with(parts, name, bit, size)
        first = jnp.where(side == 0, parts, other)
        second = jnp.where(side == 0, other, parts)
        parts = jnp.concatenate([first, second], axis=0)
    return parts


def butterfly_sum(packed, axes):
    steps = axis_steps(axes)
    if steps is None:
        return lax.psum(packed, axes)
    count = 2 ** len(steps)
    rows, cols = packed.shape
    padded = -(-rows // (8 * count)) * 8 * count
    parts = jnp.pad(packed, ((0, padded - rows), (0, 0)))
    low = 1 if len(axes) > 1 else 0
    high = len(steps) - 1
    if cols % 256 or high - low < 2:
        return run_steps(parts, steps)[:rows]
    middle = steps[low:high]
    other = steps[:low] + middle[1:] + middle[:1] + steps[high:]
    half = cols // 2
    left = run_steps(parts[:, :half], steps)
    right = run_steps(parts[:, half:], other)
    return jnp.concatenate([left, right], axis=1)[:rows]


def small_sum(values, axes):
    steps = axis_steps(axes)
    if steps is None:
        return lax.psum(values, axes)
    for name, bit, size in steps:
        values = values + swap_with(values, name, bit, size)
    return values


def butterfly_gather(piece, name):
    size = lax.axis_size(name)
    if size & (size - 1):
        return lax.all_gather(piece, name, axis=0, tiled=False)
    parts = piece[None]
    bit = size // 2
    levels = 0
    while bit >= 1:
        side = (lax.axis_index(name) // bit) % 2
        other = swap_with(parts, name, bit, size)
        first = jnp.where(side == 0, parts, other)
        second = jnp.where(side == 0, other, parts)
        parts = jnp.concatenate([first, second], axis=0)
        bit //= 2
        levels += 1
    parts = parts.reshape((2,) * levels + piece.shape)
    order = tuple(reversed(range(levels))) + tuple(range(levels, levels + piece.ndim))
    return parts.transpose(order).reshape((size,) + piece.shape)


def split3(values):
    first = values.astype(jnp.bfloat16)
    rest = values - first.astype(jnp.float32)
    second = rest.astype(jnp.bfloat16)
    third = (rest - second.astype(jnp.float32)).astype(jnp.bfloat16)
    return jnp.concatenate([first, second, third], axis=1)


def exact_dot(lhs_bf16, rhs_f32, contract):
    cols = rhs_f32.shape[1]
    wide = lax.dot_general(
        lhs_bf16,
        split3(rhs_f32),
        ((contract, (0,)), ((), ())),
        preferred_element_type=jnp.float32,
    )
    return wide[:, :cols] + wide[:, cols : 2 * cols] + wide[:, 2 * cols :]


def shards(
    grads_fc,
    grads_ln,
    grads_emb,
    weights_fc,
    basis,
    fc_m,
    fc_v,
    ln_params,
    ln_m,
    ln_v,
    emb_weights,
    emb_m,
    emb_v,
    step_count,
):
    highest = lax.Precision.HIGHEST
    replicas = lax.axis_size("dp")
    owners = lax.axis_size("own")
    replica = lax.axis_index("dp")
    blocks = grads_fc.shape[2]
    row_count = grads_fc.shape[3]
    width = grads_fc.shape[4]
    rank_cols = basis.shape[1]
    emb_count = grads_emb.shape[3]
    local_rows = grads_fc.reshape(blocks * row_count, width)
    local_proj = exact_dot(local_rows, basis, (1,))
    emb_local = grads_emb.reshape(blocks, emb_count, width).astype(jnp.float32)
    ln_local = grads_ln.reshape(4, width).astype(jnp.float32)
    proj_own, emb_own, ln_sum = unpack_rows(
        butterfly_sum(pack_rows((local_proj, emb_local, ln_local), rank_cols), ("dp",)),
        (local_proj, emb_local, ln_local),
    )
    partial_value = exact_dot(local_rows, proj_own, (0,))
    own_square = jnp.sum(proj_own * proj_own) + jnp.sum(emb_own * emb_own)
    square_total = small_sum(jnp.full((8, 128), own_square), ("own",))[0, 0]
    grad_norm = jnp.sqrt(square_total + jnp.sum(ln_sum * ln_sum) + 1e-06)
    clip_limit = math.sqrt(FF * RANK + emb_count * replicas * owners * width + 4 * width)
    factor = jnp.minimum(1.0, clip_limit / grad_norm)
    count = step_count[0].astype(jnp.float32)
    correct_one = 1.0 - jnp.power(jnp.float32(beta_one), count)
    correct_two = 1.0 - jnp.power(jnp.float32(beta_two), count)
    proj_rows = lax.dynamic_slice_in_dim(proj_own, replica * row_count, row_count, 0)
    fc_grad = factor * proj_rows.reshape(1, 1, row_count, rank_cols)
    fc_m_next, fc_v_next, fc_direction = adam_update(fc_m, fc_v, fc_grad, correct_one, correct_two)
    ln_m_next, ln_v_next, ln_direction = adam_update(
        ln_m, ln_v, factor * ln_sum, correct_one, correct_two
    )
    ln_next = ln_params - learn_rate * ln_direction
    emb_rows = lax.dynamic_index_in_dim(emb_own, replica, 0, keepdims=True).reshape(
        1, 1, emb_count, width
    )
    emb_m_next, emb_v_next, emb_direction = adam_update(
        emb_m, emb_v, factor * emb_rows, correct_one, correct_two
    )
    fc_dir_mine = fc_direction.reshape(row_count, rank_cols).astype(jnp.bfloat16)
    emb_dir_f32 = emb_direction.reshape(emb_count, width)
    emb_dir_high = emb_dir_f32.astype(jnp.bfloat16)
    emb_dir_low = (emb_dir_f32 - emb_dir_high.astype(jnp.float32)).astype(jnp.bfloat16)
    emb_dir_mine = jnp.stack([emb_dir_high, emb_dir_low])
    gathered = butterfly_gather(pack_rows((fc_dir_mine, emb_dir_mine), rank_cols), "dp")
    fc_dir_all, emb_dir_all = jax.vmap(
        lambda packed: unpack_rows(packed, (fc_dir_mine, emb_dir_mine))
    )(gathered)
    fc_dir_all = fc_dir_all.reshape(replicas * row_count, rank_cols)
    emb_dir_all = emb_dir_all[:, 0].astype(jnp.float32) + emb_dir_all[:, 1].astype(jnp.float32)
    pieces = split3(basis)
    stacked = jnp.concatenate(
        [pieces[:, :rank_cols], pieces[:, rank_cols : 2 * rank_cols], pieces[:, 2 * rank_cols :]], axis=1
    )
    update_rows = lax.dot_general(
        jnp.concatenate([fc_dir_all] * 3, axis=1),
        stacked,
        (((1,), (1,)), ((), ())),
        preferred_element_type=jnp.float32,
    )
    weights_next = (
        weights_fc.astype(jnp.float32)
        - learn_rate * galore_scale * update_rows.reshape(weights_fc.shape)
    ).astype(jnp.bfloat16)
    emb_next = (
        emb_weights.astype(jnp.float32) - learn_rate * emb_dir_all.reshape(emb_weights.shape)
    ).astype(jnp.bfloat16)
    subspace = butterfly_sum(partial_value, ("own", "dp"))
    basis_next = orthogonalize(subspace)
    return (
        fc_m_next,
        fc_v_next,
        fc_direction,
        weights_next,
        basis_next,
        ln_next,
        ln_m_next,
        ln_v_next,
        emb_next,
        emb_m_next,
        emb_v_next,
    )


def solution(mesh):
    in_specs = (
        P("dp", "own", None, None, None),
        P("dp", None, None),
        P("dp", "own", None, None, None),
        P("own", None, None, None),
        P(),
        P("own", "dp", None, None),
        P("own", "dp", None, None),
        P(),
        P(),
        P(),
        P("own", None, None, None),
        P("own", "dp", None, None),
        P("own", "dp", None, None),
        P(),
    )
    out_specs = (
        P("own", "dp", None, None),
        P("own", "dp", None, None),
        P("own", "dp", None, None),
        P("own", None, None, None),
        P(),
        P(),
        P(),
        P(),
        P("own", None, None, None),
        P("own", "dp", None, None),
        P("own", "dp", None, None),
    )
    return jax.shard_map(shards, mesh=mesh, in_specs=in_specs, out_specs=out_specs, check_vma=False)
```

```python
import math

import jax
import jax.numpy as jnp
from jax import lax
from jax.sharding import PartitionSpec as P

FF = 6400
RANK = 256
NS_STEPS = 5


beta_one = 0.9
beta_two = 0.999
adam_eps = 1e-08
learn_rate = 0.02
galore_scale = 0.25


def adam_update(moment_one, moment_two, gradient, correct_one, correct_two):
    moment_one_new = beta_one * moment_one + (1.0 - beta_one) * gradient
    moment_two_new = beta_two * moment_two + (1.0 - beta_two) * gradient * gradient
    direction = moment_one_new / correct_one / (jnp.sqrt(moment_two_new / correct_two) + adam_eps)
    return (moment_one_new, moment_two_new, direction)


def orthogonalize(subspace):
    highest = lax.Precision.HIGH
    iterate = subspace * lax.rsqrt(jnp.sum(subspace * subspace) + 1e-06)
    for sweep_index in range(NS_STEPS):
        gram_matrix = jnp.dot(iterate.T, iterate, precision=highest)
        iterate = 1.5 * iterate - 0.5 * jnp.dot(iterate, gram_matrix, precision=highest)
    return iterate


def row_count_of(piece, cols):
    return -(-piece.size // cols)


def pack_rows(pieces, cols):
    rows = []
    for piece in pieces:
        if piece.ndim == 2 and piece.shape[1] == cols:
            rows.append(piece)
            continue
        flat = piece.reshape(-1)
        flat = jnp.pad(flat, (0, row_count_of(piece, cols) * cols - flat.size))
        rows.append(flat.reshape(-1, cols))
    return jnp.concatenate(rows, axis=0)


def unpack_rows(packed, pieces):
    cols = packed.shape[1]
    out = []
    start = 0
    for piece in pieces:
        count = row_count_of(piece, cols)
        block = packed[start : start + count]
        start += count
        out.append(block.reshape(-1)[: piece.size].reshape(piece.shape))
    return out


def axis_steps(axes):
    steps = []
    for name in axes:
        size = lax.axis_size(name)
        if size & (size - 1):
            return None
        bit = 1
        while bit < size:
            steps.append((name, bit, size))
            bit *= 2
    return steps


def swap_with(values, name, bit, size):
    return lax.ppermute(values, name, [(index, index ^ bit) for index in range(size)])


def run_steps(parts, steps):
    sides = []
    for name, bit, size in steps:
        side = (lax.axis_index(name) // bit) % 2
        half = parts.shape[0] // 2
        keep = lax.dynamic_slice_in_dim(parts, side * half, half, 0)
        send = lax.dynamic_slice_in_dim(parts, (1 - side) * half, half, 0)
        parts = keep + swap_with(send, name, bit, size)
        sides.append(side)
    for (name, bit, size), side in zip(reversed(steps), reversed(sides)):
        other = swap_with(parts, name, bit, size)
        first = jnp.where(side == 0, parts, other)
        second = jnp.where(side == 0, other, parts)
        parts = jnp.concatenate([first, second], axis=0)
    return parts


def half_orders(axes):
    steps = axis_steps(axes)
    if steps is None:
        return None
    low = 1 if len(axes) > 1 else 0
    high = len(steps) - 1
    if high - low < 2:
        return steps, steps
    middle = steps[low:high]
    return steps, steps[:low] + middle[1:] + middle[:1] + steps[high:]


def half_sum(piece, axes, which):
    orders = half_orders(axes)
    if orders is None:
        return lax.psum(piece, axes)
    steps = orders[which]
    count = 2 ** len(steps)
    rows = piece.shape[0]
    padded = -(-rows // (8 * count)) * 8 * count
    return run_steps(jnp.pad(piece, ((0, padded - rows), (0, 0))), steps)[:rows]


def butterfly_sum(packed, axes):
    steps = axis_steps(axes)
    if steps is None:
        return lax.psum(packed, axes)
    count = 2 ** len(steps)
    rows, cols = packed.shape
    padded = -(-rows // (8 * count)) * 8 * count
    parts = jnp.pad(packed, ((0, padded - rows), (0, 0)))
    low = 1 if len(axes) > 1 else 0
    high = len(steps) - 1
    if cols % 256 or high - low < 2:
        return run_steps(parts, steps)[:rows]
    middle = steps[low:high]
    other = steps[:low] + middle[1:] + middle[:1] + steps[high:]
    half = cols // 2
    left = run_steps(parts[:, :half], steps)
    right = run_steps(parts[:, half:], other)
    return jnp.concatenate([left, right], axis=1)[:rows]


def small_sum(values, axes):
    steps = axis_steps(axes)
    if steps is None:
        return lax.psum(values, axes)
    for name, bit, size in steps:
        values = values + swap_with(values, name, bit, size)
    return values


def butterfly_gather(piece, name):
    size = lax.axis_size(name)
    if size & (size - 1):
        return lax.all_gather(piece, name, axis=0, tiled=False)
    parts = piece[None]
    bit = size // 2
    levels = 0
    while bit >= 1:
        side = (lax.axis_index(name) // bit) % 2
        other = swap_with(parts, name, bit, size)
        first = jnp.where(side == 0, parts, other)
        second = jnp.where(side == 0, other, parts)
        parts = jnp.concatenate([first, second], axis=0)
        bit //= 2
        levels += 1
    parts = parts.reshape((2,) * levels + piece.shape)
    order = tuple(reversed(range(levels))) + tuple(range(levels, levels + piece.ndim))
    return parts.transpose(order).reshape((size,) + piece.shape)


def split2(values):
    first = values.astype(jnp.bfloat16)
    second = (values - first.astype(jnp.float32)).astype(jnp.bfloat16)
    return jnp.concatenate([first, second], axis=1)


def exact_dot(lhs_bf16, rhs_f32, contract):
    cols = rhs_f32.shape[1]
    wide = lax.dot_general(
        lhs_bf16,
        split2(rhs_f32),
        ((contract, (0,)), ((), ())),
        preferred_element_type=jnp.float32,
    )
    return wide[:, :cols] + wide[:, cols:]


def shards(
    grads_fc,
    grads_ln,
    grads_emb,
    weights_fc,
    basis,
    fc_m,
    fc_v,
    ln_params,
    ln_m,
    ln_v,
    emb_weights,
    emb_m,
    emb_v,
    step_count,
):
    highest = lax.Precision.HIGHEST
    replicas = lax.axis_size("dp")
    owners = lax.axis_size("own")
    replica = lax.axis_index("dp")
    blocks = grads_fc.shape[2]
    row_count = grads_fc.shape[3]
    width = grads_fc.shape[4]
    rank_cols = basis.shape[1]
    emb_count = grads_emb.shape[3]
    local_rows = grads_fc.reshape(blocks * row_count, width)
    emb_local = grads_emb.reshape(blocks, emb_count, width).astype(jnp.float32)
    ln_local = grads_ln.reshape(4, width).astype(jnp.float32)
    half = rank_cols // 2
    small = pack_rows((emb_local, ln_local), half)
    small_rows = -(-small.shape[0] // 2)
    small = jnp.pad(small, ((0, 2 * small_rows - small.shape[0]), (0, 0)))
    proj_halves, small_halves, value_halves = [], [], []
    for which in range(2):
        proj_half = exact_dot(local_rows, basis[:, which * half : (which + 1) * half], (1,))
        summed = half_sum(
            jnp.concatenate([proj_half, small[which * small_rows : (which + 1) * small_rows]]),
            ("dp",),
            which,
        )
        proj_halves.append(summed[: proj_half.shape[0]])
        small_halves.append(summed[proj_half.shape[0] :])
        value_halves.append(exact_dot(local_rows, proj_halves[-1], (0,)))
    proj_own = jnp.concatenate(proj_halves, axis=1)
    emb_own, ln_sum = unpack_rows(jnp.concatenate(small_halves), (emb_local, ln_local))
    own_square = jnp.sum(proj_own * proj_own) + jnp.sum(emb_own * emb_own)
    square_total = small_sum(jnp.full((8, 128), own_square), ("own",))[0, 0]
    grad_norm = jnp.sqrt(square_total + jnp.sum(ln_sum * ln_sum) + 1e-06)
    clip_limit = math.sqrt(FF * RANK + emb_count * replicas * owners * width + 4 * width)
    factor = jnp.minimum(1.0, clip_limit / grad_norm)
    count = step_count[0].astype(jnp.float32)
    correct_one = 1.0 - jnp.power(jnp.float32(beta_one), count)
    correct_two = 1.0 - jnp.power(jnp.float32(beta_two), count)
    proj_rows = lax.dynamic_slice_in_dim(proj_own, replica * row_count, row_count, 0)
    fc_grad = factor * proj_rows.reshape(1, 1, row_count, rank_cols)
    fc_m_next, fc_v_next, fc_direction = adam_update(fc_m, fc_v, fc_grad, correct_one, correct_two)
    ln_m_next, ln_v_next, ln_direction = adam_update(
        ln_m, ln_v, factor * ln_sum, correct_one, correct_two
    )
    ln_next = ln_params - learn_rate * ln_direction
    emb_rows = lax.dynamic_index_in_dim(emb_own, replica, 0, keepdims=True).reshape(
        1, 1, emb_count, width
    )
    emb_m_next, emb_v_next, emb_direction = adam_update(
        emb_m, emb_v, factor * emb_rows, correct_one, correct_two
    )
    fc_dir_mine = fc_direction.reshape(row_count, rank_cols).astype(jnp.bfloat16)
    emb_dir_f32 = emb_direction.reshape(emb_count, width)
    emb_dir_high = emb_dir_f32.astype(jnp.bfloat16)
    emb_dir_low = (emb_dir_f32 - emb_dir_high.astype(jnp.float32)).astype(jnp.bfloat16)
    emb_dir_mine = jnp.stack([emb_dir_high, emb_dir_low])
    gathered = butterfly_gather(pack_rows((fc_dir_mine, emb_dir_mine), rank_cols), "dp")
    fc_dir_all, emb_dir_all = jax.vmap(
        lambda packed: unpack_rows(packed, (fc_dir_mine, emb_dir_mine))
    )(gathered)
    fc_dir_all = fc_dir_all.reshape(replicas * row_count, rank_cols)
    emb_dir_all = emb_dir_all[:, 0].astype(jnp.float32) + emb_dir_all[:, 1].astype(jnp.float32)
    update_rows = lax.dot_general(
        jnp.concatenate([fc_dir_all] * 2, axis=1),
        split2(basis),
        (((1,), (1,)), ((), ())),
        preferred_element_type=jnp.float32,
    )
    weights_next = (
        weights_fc.astype(jnp.float32)
        - learn_rate * galore_scale * update_rows.reshape(weights_fc.shape)
    ).astype(jnp.bfloat16)
    emb_next = (
        emb_weights.astype(jnp.float32) - learn_rate * emb_dir_all.reshape(emb_weights.shape)
    ).astype(jnp.bfloat16)
    subspace = jnp.concatenate(
        [half_sum(value_halves[which], ("own", "dp"), which) for which in range(2)], axis=1
    )
    basis_next = orthogonalize(subspace)
    return (
        fc_m_next,
        fc_v_next,
        fc_direction,
        weights_next,
        basis_next,
        ln_next,
        ln_m_next,
        ln_v_next,
        emb_next,
        emb_m_next,
        emb_v_next,
    )


def solution(mesh):
    in_specs = (
        P("dp", "own", None, None, None),
        P("dp", None, None),
        P("dp", "own", None, None, None),
        P("own", None, None, None),
        P(),
        P("own", "dp", None, None),
        P("own", "dp", None, None),
        P(),
        P(),
        P(),
        P("own", None, None, None),
        P("own", "dp", None, None),
        P("own", "dp", None, None),
        P(),
    )
    out_specs = (
        P("own", "dp", None, None),
        P("own", "dp", None, None),
        P("own", "dp", None, None),
        P("own", None, None, None),
        P(),
        P(),
        P(),
        P(),
        P("own", None, None, None),
        P("own", "dp", None, None),
        P("own", "dp", None, None),
    )
    return jax.shard_map(shards, mesh=mesh, in_specs=in_specs, out_specs=out_specs, check_vma=False)
```

```python
import math

import jax
import jax.numpy as jnp
from jax import lax
from jax.experimental import pallas as pl
from jax.sharding import PartitionSpec as P

FF = 6400
RANK = 256
NS_STEPS = 5


beta_one = 0.9
beta_two = 0.999
adam_eps = 1e-08
learn_rate = 0.02
galore_scale = 0.25


def adam_update(moment_one, moment_two, gradient, correct_one, correct_two):
    moment_one_new = beta_one * moment_one + (1.0 - beta_one) * gradient
    moment_two_new = beta_two * moment_two + (1.0 - beta_two) * gradient * gradient
    direction = moment_one_new / correct_one / (jnp.sqrt(moment_two_new / correct_two) + adam_eps)
    return (moment_one_new, moment_two_new, direction)


def orthogonalize(subspace):
    highest = lax.Precision.HIGH
    iterate = subspace * lax.rsqrt(jnp.sum(subspace * subspace) + 1e-06)
    for sweep_index in range(NS_STEPS):
        gram_matrix = jnp.dot(iterate.T, iterate, precision=highest)
        iterate = 1.5 * iterate - 0.5 * jnp.dot(iterate, gram_matrix, precision=highest)
    return iterate


def row_count_of(piece, cols):
    return -(-piece.size // cols)


def pack_rows(pieces, cols):
    rows = []
    for piece in pieces:
        if piece.ndim == 2 and piece.shape[1] == cols:
            rows.append(piece)
            continue
        flat = piece.reshape(-1)
        flat = jnp.pad(flat, (0, row_count_of(piece, cols) * cols - flat.size))
        rows.append(flat.reshape(-1, cols))
    return jnp.concatenate(rows, axis=0)


def unpack_rows(packed, pieces):
    cols = packed.shape[1]
    out = []
    start = 0
    for piece in pieces:
        count = row_count_of(piece, cols)
        block = packed[start : start + count]
        start += count
        out.append(block.reshape(-1)[: piece.size].reshape(piece.shape))
    return out


def axis_steps(axes):
    steps = []
    for name in axes:
        size = lax.axis_size(name)
        if size & (size - 1):
            return None
        bit = 1
        while bit < size:
            steps.append((name, bit, size))
            bit *= 2
    return steps


def swap_with(values, name, bit, size):
    return lax.ppermute(values, name, [(index, index ^ bit) for index in range(size)])


def run_steps(parts, steps):
    sides = []
    for name, bit, size in steps:
        side = (lax.axis_index(name) // bit) % 2
        half = parts.shape[0] // 2
        keep = lax.dynamic_slice_in_dim(parts, side * half, half, 0)
        send = lax.dynamic_slice_in_dim(parts, (1 - side) * half, half, 0)
        parts = keep + swap_with(send, name, bit, size)
        sides.append(side)
    for (name, bit, size), side in zip(reversed(steps), reversed(sides)):
        other = swap_with(parts, name, bit, size)
        first = jnp.where(side == 0, parts, other)
        second = jnp.where(side == 0, other, parts)
        parts = jnp.concatenate([first, second], axis=0)
    return parts


def half_orders(axes):
    steps = axis_steps(axes)
    if steps is None:
        return None
    low = 1 if len(axes) > 1 else 0
    high = len(steps) - 1
    if high - low < 2:
        return steps, steps
    middle = steps[low:high]
    return steps, steps[:low] + middle[1:] + middle[:1] + steps[high:]


def half_sum(piece, axes, which):
    orders = half_orders(axes)
    if orders is None:
        return lax.psum(piece, axes)
    steps = orders[which]
    count = 2 ** len(steps)
    rows = piece.shape[0]
    padded = -(-rows // (8 * count)) * 8 * count
    return run_steps(jnp.pad(piece, ((0, padded - rows), (0, 0))), steps)[:rows]


def butterfly_sum(packed, axes):
    steps = axis_steps(axes)
    if steps is None:
        return lax.psum(packed, axes)
    count = 2 ** len(steps)
    rows, cols = packed.shape
    padded = -(-rows // (8 * count)) * 8 * count
    parts = jnp.pad(packed, ((0, padded - rows), (0, 0)))
    low = 1 if len(axes) > 1 else 0
    high = len(steps) - 1
    if cols % 256 or high - low < 2:
        return run_steps(parts, steps)[:rows]
    middle = steps[low:high]
    other = steps[:low] + middle[1:] + middle[:1] + steps[high:]
    half = cols // 2
    left = run_steps(parts[:, :half], steps)
    right = run_steps(parts[:, half:], other)
    return jnp.concatenate([left, right], axis=1)[:rows]


def small_sum(values, axes):
    steps = axis_steps(axes)
    if steps is None:
        return lax.psum(values, axes)
    for name, bit, size in steps:
        values = values + swap_with(values, name, bit, size)
    return values


def butterfly_gather(piece, name):
    size = lax.axis_size(name)
    if size & (size - 1):
        return lax.all_gather(piece, name, axis=0, tiled=False)
    parts = piece[None]
    bit = size // 2
    levels = 0
    while bit >= 1:
        side = (lax.axis_index(name) // bit) % 2
        other = swap_with(parts, name, bit, size)
        first = jnp.where(side == 0, parts, other)
        second = jnp.where(side == 0, other, parts)
        parts = jnp.concatenate([first, second], axis=0)
        bit //= 2
        levels += 1
    parts = parts.reshape((2,) * levels + piece.shape)
    order = tuple(reversed(range(levels))) + tuple(range(levels, levels + piece.ndim))
    return parts.transpose(order).reshape((size,) + piece.shape)


def update_kernel(direction_ref, basis_ref, weight_ref, out_ref):
    update = lax.dot_general(
        direction_ref[0],
        basis_ref[...],
        (((1,), (1,)), ((), ())),
        preferred_element_type=jnp.float32,
    )
    out_ref[0] = (
        weight_ref[0].astype(jnp.float32) - learn_rate * galore_scale * update
    ).astype(out_ref.dtype)


def updated_weights(direction_bf16, basis, weights):
    blocks, rows, width = weights.shape
    pieces = split2(basis)
    depth = pieces.shape[1]
    doubled = jnp.concatenate([direction_bf16] * 2, axis=1).reshape(blocks, rows, depth)
    return pl.pallas_call(
        update_kernel,
        out_shape=jax.ShapeDtypeStruct(weights.shape, jnp.bfloat16),
        grid=(blocks,),
        in_specs=[
            pl.BlockSpec((1, rows, depth), lambda index: (index, 0, 0)),
            pl.BlockSpec((width, depth), lambda index: (0, 0)),
            pl.BlockSpec((1, rows, width), lambda index: (index, 0, 0)),
        ],
        out_specs=pl.BlockSpec((1, rows, width), lambda index: (index, 0, 0)),
    )(doubled, pieces, weights)


def split2(values):
    first = values.astype(jnp.bfloat16)
    second = (values - first.astype(jnp.float32)).astype(jnp.bfloat16)
    return jnp.concatenate([first, second], axis=1)


def exact_dot(lhs_bf16, rhs_f32, contract):
    cols = rhs_f32.shape[1]
    wide = lax.dot_general(
        lhs_bf16,
        split2(rhs_f32),
        ((contract, (0,)), ((), ())),
        preferred_element_type=jnp.float32,
    )
    return wide[:, :cols] + wide[:, cols:]


def shards(
    grads_fc,
    grads_ln,
    grads_emb,
    weights_fc,
    basis,
    fc_m,
    fc_v,
    ln_params,
    ln_m,
    ln_v,
    emb_weights,
    emb_m,
    emb_v,
    step_count,
):
    highest = lax.Precision.HIGHEST
    replicas = lax.axis_size("dp")
    owners = lax.axis_size("own")
    replica = lax.axis_index("dp")
    blocks = grads_fc.shape[2]
    row_count = grads_fc.shape[3]
    width = grads_fc.shape[4]
    rank_cols = basis.shape[1]
    emb_count = grads_emb.shape[3]
    local_rows = grads_fc.reshape(blocks * row_count, width)
    emb_local = grads_emb.reshape(blocks, emb_count, width).astype(jnp.float32)
    ln_local = grads_ln.reshape(4, width).astype(jnp.float32)
    half = rank_cols // 2
    small = pack_rows((emb_local, ln_local), half)
    small_rows = -(-small.shape[0] // 2)
    small = jnp.pad(small, ((0, 2 * small_rows - small.shape[0]), (0, 0)))
    proj_halves, small_halves, value_halves = [], [], []
    for which in range(2):
        proj_half = exact_dot(local_rows, basis[:, which * half : (which + 1) * half], (1,))
        summed = half_sum(
            jnp.concatenate([proj_half, small[which * small_rows : (which + 1) * small_rows]]),
            ("dp",),
            which,
        )
        proj_halves.append(summed[: proj_half.shape[0]])
        small_halves.append(summed[proj_half.shape[0] :])
        value_halves.append(exact_dot(local_rows, proj_halves[-1], (0,)))
    proj_own = jnp.concatenate(proj_halves, axis=1)
    emb_own, ln_sum = unpack_rows(jnp.concatenate(small_halves), (emb_local, ln_local))
    own_square = jnp.sum(proj_own * proj_own) + jnp.sum(emb_own * emb_own)
    square_total = small_sum(jnp.full((8, 128), own_square), ("own",))[0, 0]
    grad_norm = jnp.sqrt(square_total + jnp.sum(ln_sum * ln_sum) + 1e-06)
    clip_limit = math.sqrt(FF * RANK + emb_count * replicas * owners * width + 4 * width)
    factor = jnp.minimum(1.0, clip_limit / grad_norm)
    count = step_count[0].astype(jnp.float32)
    correct_one = 1.0 - jnp.power(jnp.float32(beta_one), count)
    correct_two = 1.0 - jnp.power(jnp.float32(beta_two), count)
    proj_rows = lax.dynamic_slice_in_dim(proj_own, replica * row_count, row_count, 0)
    fc_grad = factor * proj_rows.reshape(1, 1, row_count, rank_cols)
    fc_m_next, fc_v_next, fc_direction = adam_update(fc_m, fc_v, fc_grad, correct_one, correct_two)
    ln_m_next, ln_v_next, ln_direction = adam_update(
        ln_m, ln_v, factor * ln_sum, correct_one, correct_two
    )
    ln_next = ln_params - learn_rate * ln_direction
    emb_rows = lax.dynamic_index_in_dim(emb_own, replica, 0, keepdims=True).reshape(
        1, 1, emb_count, width
    )
    emb_m_next, emb_v_next, emb_direction = adam_update(
        emb_m, emb_v, factor * emb_rows, correct_one, correct_two
    )
    fc_dir_mine = fc_direction.reshape(row_count, rank_cols).astype(jnp.bfloat16)
    emb_dir_f32 = emb_direction.reshape(emb_count, width)
    emb_dir_high = emb_dir_f32.astype(jnp.bfloat16)
    emb_dir_low = (emb_dir_f32 - emb_dir_high.astype(jnp.float32)).astype(jnp.bfloat16)
    emb_dir_mine = jnp.stack([emb_dir_high, emb_dir_low])
    gathered = butterfly_gather(pack_rows((fc_dir_mine, emb_dir_mine), rank_cols), "dp")
    fc_dir_all, emb_dir_all = jax.vmap(
        lambda packed: unpack_rows(packed, (fc_dir_mine, emb_dir_mine))
    )(gathered)
    fc_dir_all = fc_dir_all.reshape(replicas * row_count, rank_cols)
    emb_dir_all = emb_dir_all[:, 0].astype(jnp.float32) + emb_dir_all[:, 1].astype(jnp.float32)
    weights_next = updated_weights(fc_dir_all, basis, weights_fc[0]).reshape(weights_fc.shape)
    emb_next = (
        emb_weights.astype(jnp.float32) - learn_rate * emb_dir_all.reshape(emb_weights.shape)
    ).astype(jnp.bfloat16)
    subspace = jnp.concatenate(
        [half_sum(value_halves[which], ("own", "dp"), which) for which in range(2)], axis=1
    )
    basis_next = orthogonalize(subspace)
    return (
        fc_m_next,
        fc_v_next,
        fc_direction,
        weights_next,
        basis_next,
        ln_next,
        ln_m_next,
        ln_v_next,
        emb_next,
        emb_m_next,
        emb_v_next,
    )


def solution(mesh):
    in_specs = (
        P("dp", "own", None, None, None),
        P("dp", None, None),
        P("dp", "own", None, None, None),
        P("own", None, None, None),
        P(),
        P("own", "dp", None, None),
        P("own", "dp", None, None),
        P(),
        P(),
        P(),
        P("own", None, None, None),
        P("own", "dp", None, None),
        P("own", "dp", None, None),
        P(),
    )
    out_specs = (
        P("own", "dp", None, None),
        P("own", "dp", None, None),
        P("own", "dp", None, None),
        P("own", None, None, None),
        P(),
        P(),
        P(),
        P(),
        P("own", None, None, None),
        P("own", "dp", None, None),
        P("own", "dp", None, None),
    )
    return jax.shard_map(shards, mesh=mesh, in_specs=in_specs, out_specs=out_specs, check_vma=False)
```

```python
import math

import jax
import jax.numpy as jnp
from jax import lax
from jax.experimental import pallas as pl
from jax.sharding import PartitionSpec as P

FF = 6400
RANK = 256
NS_STEPS = 5


beta_one = 0.9
beta_two = 0.999
adam_eps = 1e-08
learn_rate = 0.02
galore_scale = 0.25


def adam_update(moment_one, moment_two, gradient, correct_one, correct_two):
    moment_one_new = beta_one * moment_one + (1.0 - beta_one) * gradient
    moment_two_new = beta_two * moment_two + (1.0 - beta_two) * gradient * gradient
    direction = moment_one_new / correct_one / (jnp.sqrt(moment_two_new / correct_two) + adam_eps)
    return (moment_one_new, moment_two_new, direction)


def orthogonalize(subspace):
    highest = lax.Precision.HIGH
    iterate = subspace * lax.rsqrt(jnp.sum(subspace * subspace) + 1e-06)
    for sweep_index in range(NS_STEPS):
        gram_matrix = jnp.dot(iterate.T, iterate, precision=highest)
        iterate = 1.5 * iterate - 0.5 * jnp.dot(iterate, gram_matrix, precision=highest)
    return iterate


def row_count_of(piece, cols):
    return -(-piece.size // cols)


def pack_rows(pieces, cols):
    rows = []
    for piece in pieces:
        if piece.ndim == 2 and piece.shape[1] == cols:
            rows.append(piece)
            continue
        flat = piece.reshape(-1)
        flat = jnp.pad(flat, (0, row_count_of(piece, cols) * cols - flat.size))
        rows.append(flat.reshape(-1, cols))
    return jnp.concatenate(rows, axis=0)


def unpack_rows(packed, pieces):
    cols = packed.shape[1]
    out = []
    start = 0
    for piece in pieces:
        count = row_count_of(piece, cols)
        block = packed[start : start + count]
        start += count
        out.append(block.reshape(-1)[: piece.size].reshape(piece.shape))
    return out


def axis_steps(axes):
    steps = []
    for name in axes:
        size = lax.axis_size(name)
        if size & (size - 1):
            return None
        bit = 1
        while bit < size:
            steps.append((name, bit, size))
            bit *= 2
    return steps


def swap_with(values, name, bit, size):
    return lax.ppermute(values, name, [(index, index ^ bit) for index in range(size)])


def run_steps(parts, steps):
    sides = []
    for name, bit, size in steps:
        side = (lax.axis_index(name) // bit) % 2
        half = parts.shape[0] // 2
        keep = lax.dynamic_slice_in_dim(parts, side * half, half, 0)
        send = lax.dynamic_slice_in_dim(parts, (1 - side) * half, half, 0)
        parts = keep + swap_with(send, name, bit, size)
        sides.append(side)
    for (name, bit, size), side in zip(reversed(steps), reversed(sides)):
        other = swap_with(parts, name, bit, size)
        first = jnp.where(side == 0, parts, other)
        second = jnp.where(side == 0, other, parts)
        parts = jnp.concatenate([first, second], axis=0)
    return parts


def half_orders(axes):
    steps = axis_steps(axes)
    if steps is None:
        return None
    low = 1 if len(axes) > 1 else 0
    high = len(steps) - 1
    if high - low < 2:
        return steps, steps
    middle = steps[low:high]
    return steps, steps[:low] + middle[1:] + middle[:1] + steps[high:]


def half_sum(piece, axes, which):
    orders = half_orders(axes)
    if orders is None:
        return lax.psum(piece, axes)
    steps = orders[which]
    count = 2 ** len(steps)
    rows = piece.shape[0]
    padded = -(-rows // (8 * count)) * 8 * count
    return run_steps(jnp.pad(piece, ((0, padded - rows), (0, 0))), steps)[:rows]


def butterfly_sum(packed, axes):
    steps = axis_steps(axes)
    if steps is None:
        return lax.psum(packed, axes)
    count = 2 ** len(steps)
    rows, cols = packed.shape
    padded = -(-rows // (8 * count)) * 8 * count
    parts = jnp.pad(packed, ((0, padded - rows), (0, 0)))
    low = 1 if len(axes) > 1 else 0
    high = len(steps) - 1
    if cols % 256 or high - low < 2:
        return run_steps(parts, steps)[:rows]
    middle = steps[low:high]
    other = steps[:low] + middle[1:] + middle[:1] + steps[high:]
    half = cols // 2
    left = run_steps(parts[:, :half], steps)
    right = run_steps(parts[:, half:], other)
    return jnp.concatenate([left, right], axis=1)[:rows]


def small_sum(values, axes):
    steps = axis_steps(axes)
    if steps is None:
        return lax.psum(values, axes)
    for name, bit, size in steps:
        values = values + swap_with(values, name, bit, size)
    return values


def butterfly_gather(piece, name):
    size = lax.axis_size(name)
    if size & (size - 1):
        return lax.all_gather(piece, name, axis=0, tiled=False)
    parts = piece[None]
    bit = size // 2
    levels = 0
    while bit >= 1:
        side = (lax.axis_index(name) // bit) % 2
        other = swap_with(parts, name, bit, size)
        first = jnp.where(side == 0, parts, other)
        second = jnp.where(side == 0, other, parts)
        parts = jnp.concatenate([first, second], axis=0)
        bit //= 2
        levels += 1
    parts = parts.reshape((2,) * levels + piece.shape)
    order = tuple(reversed(range(levels))) + tuple(range(levels, levels + piece.ndim))
    return parts.transpose(order).reshape((size,) + piece.shape)


def update_kernel(direction_ref, basis_ref, weight_ref, out_ref):
    update = lax.dot_general(
        direction_ref[0],
        basis_ref[...],
        (((1,), (0,)), ((), ())),
        preferred_element_type=jnp.float32,
    )
    out_ref[0] = (
        weight_ref[0].astype(jnp.float32) - learn_rate * galore_scale * update
    ).astype(out_ref.dtype)


def updated_weights(direction_bf16, basis, weights):
    blocks, rows, width = weights.shape
    pieces = split2(basis).T
    depth = pieces.shape[0]
    doubled = jnp.concatenate([direction_bf16] * 2, axis=1).reshape(blocks, rows, depth)
    return pl.pallas_call(
        update_kernel,
        out_shape=jax.ShapeDtypeStruct(weights.shape, jnp.bfloat16),
        grid=(blocks,),
        in_specs=[
            pl.BlockSpec((1, rows, depth), lambda index: (index, 0, 0)),
            pl.BlockSpec((depth, width), lambda index: (0, 0)),
            pl.BlockSpec((1, rows, width), lambda index: (index, 0, 0)),
        ],
        out_specs=pl.BlockSpec((1, rows, width), lambda index: (index, 0, 0)),
    )(doubled, pieces, weights)


def split2(values):
    first = values.astype(jnp.bfloat16)
    second = (values - first.astype(jnp.float32)).astype(jnp.bfloat16)
    return jnp.concatenate([first, second], axis=1)


def exact_dot(lhs_bf16, rhs_f32, contract):
    cols = rhs_f32.shape[1]
    wide = lax.dot_general(
        lhs_bf16,
        split2(rhs_f32),
        ((contract, (0,)), ((), ())),
        preferred_element_type=jnp.float32,
    )
    return wide[:, :cols] + wide[:, cols:]


def shards(
    grads_fc,
    grads_ln,
    grads_emb,
    weights_fc,
    basis,
    fc_m,
    fc_v,
    ln_params,
    ln_m,
    ln_v,
    emb_weights,
    emb_m,
    emb_v,
    step_count,
):
    highest = lax.Precision.HIGHEST
    replicas = lax.axis_size("dp")
    owners = lax.axis_size("own")
    replica = lax.axis_index("dp")
    blocks = grads_fc.shape[2]
    row_count = grads_fc.shape[3]
    width = grads_fc.shape[4]
    rank_cols = basis.shape[1]
    emb_count = grads_emb.shape[3]
    local_rows = grads_fc.reshape(blocks * row_count, width)
    emb_local = grads_emb.reshape(blocks, emb_count, width).astype(jnp.float32)
    ln_local = grads_ln.reshape(4, width).astype(jnp.float32)
    half = rank_cols // 2
    small = pack_rows((emb_local, ln_local), half)
    small_rows = -(-small.shape[0] // 2)
    small = jnp.pad(small, ((0, 2 * small_rows - small.shape[0]), (0, 0)))
    proj_halves, small_halves, value_halves = [], [], []
    for which in range(2):
        proj_half = exact_dot(local_rows, basis[:, which * half : (which + 1) * half], (1,))
        summed = half_sum(
            jnp.concatenate([proj_half, small[which * small_rows : (which + 1) * small_rows]]),
            ("dp",),
            which,
        )
        proj_halves.append(summed[: proj_half.shape[0]])
        small_halves.append(summed[proj_half.shape[0] :])
        value_halves.append(exact_dot(local_rows, proj_halves[-1], (0,)))
    proj_own = jnp.concatenate(proj_halves, axis=1)
    emb_own, ln_sum = unpack_rows(jnp.concatenate(small_halves), (emb_local, ln_local))
    own_square = jnp.sum(proj_own * proj_own) + jnp.sum(emb_own * emb_own)
    square_total = small_sum(jnp.full((8, 128), own_square), ("own",))[0, 0]
    grad_norm = jnp.sqrt(square_total + jnp.sum(ln_sum * ln_sum) + 1e-06)
    clip_limit = math.sqrt(FF * RANK + emb_count * replicas * owners * width + 4 * width)
    factor = jnp.minimum(1.0, clip_limit / grad_norm)
    count = step_count[0].astype(jnp.float32)
    correct_one = 1.0 - jnp.power(jnp.float32(beta_one), count)
    correct_two = 1.0 - jnp.power(jnp.float32(beta_two), count)
    proj_rows = lax.dynamic_slice_in_dim(proj_own, replica * row_count, row_count, 0)
    fc_grad = factor * proj_rows.reshape(1, 1, row_count, rank_cols)
    fc_m_next, fc_v_next, fc_direction = adam_update(fc_m, fc_v, fc_grad, correct_one, correct_two)
    ln_m_next, ln_v_next, ln_direction = adam_update(
        ln_m, ln_v, factor * ln_sum, correct_one, correct_two
    )
    ln_next = ln_params - learn_rate * ln_direction
    emb_rows = lax.dynamic_index_in_dim(emb_own, replica, 0, keepdims=True).reshape(
        1, 1, emb_count, width
    )
    emb_m_next, emb_v_next, emb_direction = adam_update(
        emb_m, emb_v, factor * emb_rows, correct_one, correct_two
    )
    fc_dir_mine = fc_direction.reshape(row_count, rank_cols).astype(jnp.bfloat16)
    emb_dir_f32 = emb_direction.reshape(emb_count, width)
    emb_dir_high = emb_dir_f32.astype(jnp.bfloat16)
    emb_dir_low = (emb_dir_f32 - emb_dir_high.astype(jnp.float32)).astype(jnp.bfloat16)
    emb_dir_mine = jnp.stack([emb_dir_high, emb_dir_low])
    gathered = butterfly_gather(pack_rows((fc_dir_mine, emb_dir_mine), rank_cols), "dp")
    fc_dir_all, emb_dir_all = jax.vmap(
        lambda packed: unpack_rows(packed, (fc_dir_mine, emb_dir_mine))
    )(gathered)
    fc_dir_all = fc_dir_all.reshape(replicas * row_count, rank_cols)
    emb_dir_all = emb_dir_all[:, 0].astype(jnp.float32) + emb_dir_all[:, 1].astype(jnp.float32)
    weights_next = updated_weights(fc_dir_all, basis, weights_fc[0]).reshape(weights_fc.shape)
    emb_next = (
        emb_weights.astype(jnp.float32) - learn_rate * emb_dir_all.reshape(emb_weights.shape)
    ).astype(jnp.bfloat16)
    subspace = jnp.concatenate(
        [half_sum(value_halves[which], ("own", "dp"), which) for which in range(2)], axis=1
    )
    basis_next = orthogonalize(subspace)
    return (
        fc_m_next,
        fc_v_next,
        fc_direction,
        weights_next,
        basis_next,
        ln_next,
        ln_m_next,
        ln_v_next,
        emb_next,
        emb_m_next,
        emb_v_next,
    )


def solution(mesh):
    in_specs = (
        P("dp", "own", None, None, None),
        P("dp", None, None),
        P("dp", "own", None, None, None),
        P("own", None, None, None),
        P(),
        P("own", "dp", None, None),
        P("own", "dp", None, None),
        P(),
        P(),
        P(),
        P("own", None, None, None),
        P("own", "dp", None, None),
        P("own", "dp", None, None),
        P(),
    )
    out_specs = (
        P("own", "dp", None, None),
        P("own", "dp", None, None),
        P("own", "dp", None, None),
        P("own", None, None, None),
        P(),
        P(),
        P(),
        P(),
        P("own", None, None, None),
        P("own", "dp", None, None),
        P("own", "dp", None, None),
    )
    return jax.shard_map(shards, mesh=mesh, in_specs=in_specs, out_specs=out_specs, check_vma=False)
```

```python
import math

import jax
import jax.numpy as jnp
from jax import lax
from jax.experimental import pallas as pl
from jax.sharding import PartitionSpec as P

FF = 6400
RANK = 256
NS_STEPS = 5


beta_one = 0.9
beta_two = 0.999
adam_eps = 1e-08
learn_rate = 0.02
galore_scale = 0.25


def adam_update(moment_one, moment_two, gradient, correct_one, correct_two):
    moment_one_new = beta_one * moment_one + (1.0 - beta_one) * gradient
    moment_two_new = beta_two * moment_two + (1.0 - beta_two) * gradient * gradient
    direction = moment_one_new / correct_one / (jnp.sqrt(moment_two_new / correct_two) + adam_eps)
    return (moment_one_new, moment_two_new, direction)


def orthogonalize(subspace):
    high = lax.Precision.HIGH
    highest = lax.Precision.HIGHEST
    iterate = subspace * lax.rsqrt(jnp.sum(subspace * subspace) + 1e-06)
    gram_matrix = jnp.dot(iterate.T, iterate, precision=highest)
    identity = jnp.eye(gram_matrix.shape[0], dtype=gram_matrix.dtype)
    product = None
    for sweep_index in range(NS_STEPS):
        step = 1.5 * identity - 0.5 * gram_matrix
        product = step if product is None else jnp.dot(product, step, precision=highest)
        if sweep_index + 1 < NS_STEPS:
            gram_matrix = jnp.dot(
                step, jnp.dot(gram_matrix, step, precision=highest), precision=highest
            )
    return jnp.dot(iterate, product, precision=high)


def row_count_of(piece, cols):
    return -(-piece.size // cols)


def pack_rows(pieces, cols):
    rows = []
    for piece in pieces:
        if piece.ndim == 2 and piece.shape[1] == cols:
            rows.append(piece)
            continue
        flat = piece.reshape(-1)
        flat = jnp.pad(flat, (0, row_count_of(piece, cols) * cols - flat.size))
        rows.append(flat.reshape(-1, cols))
    return jnp.concatenate(rows, axis=0)


def unpack_rows(packed, pieces):
    cols = packed.shape[1]
    out = []
    start = 0
    for piece in pieces:
        count = row_count_of(piece, cols)
        block = packed[start : start + count]
        start += count
        out.append(block.reshape(-1)[: piece.size].reshape(piece.shape))
    return out


def axis_steps(axes):
    steps = []
    for name in axes:
        size = lax.axis_size(name)
        if size & (size - 1):
            return None
        bit = 1
        while bit < size:
            steps.append((name, bit, size))
            bit *= 2
    return steps


def swap_with(values, name, bit, size):
    return lax.ppermute(values, name, [(index, index ^ bit) for index in range(size)])


def run_steps(parts, steps):
    sides = []
    for name, bit, size in steps:
        side = (lax.axis_index(name) // bit) % 2
        half = parts.shape[0] // 2
        keep = lax.dynamic_slice_in_dim(parts, side * half, half, 0)
        send = lax.dynamic_slice_in_dim(parts, (1 - side) * half, half, 0)
        parts = keep + swap_with(send, name, bit, size)
        sides.append(side)
    for (name, bit, size), side in zip(reversed(steps), reversed(sides)):
        other = swap_with(parts, name, bit, size)
        first = jnp.where(side == 0, parts, other)
        second = jnp.where(side == 0, other, parts)
        parts = jnp.concatenate([first, second], axis=0)
    return parts


def half_orders(axes):
    steps = axis_steps(axes)
    if steps is None:
        return None
    low = 1 if len(axes) > 1 else 0
    high = len(steps) - 1
    if high - low < 2:
        return steps, steps
    middle = steps[low:high]
    return steps, steps[:low] + middle[1:] + middle[:1] + steps[high:]


def half_sum(piece, axes, which):
    orders = half_orders(axes)
    if orders is None:
        return lax.psum(piece, axes)
    steps = orders[which]
    count = 2 ** len(steps)
    rows = piece.shape[0]
    padded = -(-rows // (8 * count)) * 8 * count
    return run_steps(jnp.pad(piece, ((0, padded - rows), (0, 0))), steps)[:rows]


def butterfly_sum(packed, axes):
    steps = axis_steps(axes)
    if steps is None:
        return lax.psum(packed, axes)
    count = 2 ** len(steps)
    rows, cols = packed.shape
    padded = -(-rows // (8 * count)) * 8 * count
    parts = jnp.pad(packed, ((0, padded - rows), (0, 0)))
    low = 1 if len(axes) > 1 else 0
    high = len(steps) - 1
    if cols % 256 or high - low < 2:
        return run_steps(parts, steps)[:rows]
    middle = steps[low:high]
    other = steps[:low] + middle[1:] + middle[:1] + steps[high:]
    half = cols // 2
    left = run_steps(parts[:, :half], steps)
    right = run_steps(parts[:, half:], other)
    return jnp.concatenate([left, right], axis=1)[:rows]


def small_sum(values, axes):
    steps = axis_steps(axes)
    if steps is None:
        return lax.psum(values, axes)
    for name, bit, size in steps:
        values = values + swap_with(values, name, bit, size)
    return values


def butterfly_gather(piece, name):
    size = lax.axis_size(name)
    if size & (size - 1):
        return lax.all_gather(piece, name, axis=0, tiled=False)
    parts = piece[None]
    bit = size // 2
    levels = 0
    while bit >= 1:
        side = (lax.axis_index(name) // bit) % 2
        other = swap_with(parts, name, bit, size)
        first = jnp.where(side == 0, parts, other)
        second = jnp.where(side == 0, other, parts)
        parts = jnp.concatenate([first, second], axis=0)
        bit //= 2
        levels += 1
    parts = parts.reshape((2,) * levels + piece.shape)
    order = tuple(reversed(range(levels))) + tuple(range(levels, levels + piece.ndim))
    return parts.transpose(order).reshape((size,) + piece.shape)


def update_kernel(direction_ref, basis_ref, weight_ref, out_ref):
    for block in range(direction_ref.shape[0]):
        update = lax.dot_general(
            direction_ref[block],
            basis_ref[...],
            (((1,), (0,)), ((), ())),
            preferred_element_type=jnp.float32,
        )
        out_ref[block] = (
            weight_ref[block].astype(jnp.float32) - learn_rate * galore_scale * update
        ).astype(out_ref.dtype)


def updated_weights(direction_bf16, basis, weights):
    blocks, rows, width = weights.shape
    pieces = split2(basis).T
    depth = pieces.shape[0]
    doubled = jnp.concatenate([direction_bf16] * 2, axis=1).reshape(blocks, rows, depth)
    group = 2 if blocks % 2 == 0 else 1
    return pl.pallas_call(
        update_kernel,
        out_shape=jax.ShapeDtypeStruct(weights.shape, jnp.bfloat16),
        grid=(blocks // group,),
        in_specs=[
            pl.BlockSpec((group, rows, depth), lambda index: (index, 0, 0)),
            pl.BlockSpec((depth, width), lambda index: (0, 0)),
            pl.BlockSpec((group, rows, width), lambda index: (index, 0, 0)),
        ],
        out_specs=pl.BlockSpec((group, rows, width), lambda index: (index, 0, 0)),
    )(doubled, pieces, weights)


def split2(values):
    first = values.astype(jnp.bfloat16)
    second = (values - first.astype(jnp.float32)).astype(jnp.bfloat16)
    return jnp.concatenate([first, second], axis=1)


def exact_dot(lhs_bf16, rhs_f32, contract):
    cols = rhs_f32.shape[1]
    wide = lax.dot_general(
        lhs_bf16,
        split2(rhs_f32),
        ((contract, (0,)), ((), ())),
        preferred_element_type=jnp.float32,
    )
    return wide[:, :cols] + wide[:, cols:]


def shards(
    grads_fc,
    grads_ln,
    grads_emb,
    weights_fc,
    basis,
    fc_m,
    fc_v,
    ln_params,
    ln_m,
    ln_v,
    emb_weights,
    emb_m,
    emb_v,
    step_count,
):
    highest = lax.Precision.HIGHEST
    replicas = lax.axis_size("dp")
    owners = lax.axis_size("own")
    replica = lax.axis_index("dp")
    blocks = grads_fc.shape[2]
    row_count = grads_fc.shape[3]
    width = grads_fc.shape[4]
    rank_cols = basis.shape[1]
    emb_count = grads_emb.shape[3]
    local_rows = grads_fc.reshape(blocks * row_count, width)
    emb_local = grads_emb.reshape(blocks, emb_count, width).astype(jnp.float32)
    ln_local = grads_ln.reshape(4, width).astype(jnp.float32)
    half = rank_cols // 2
    small = pack_rows((emb_local, ln_local), half)
    small_rows = -(-small.shape[0] // 2)
    small = jnp.pad(small, ((0, 2 * small_rows - small.shape[0]), (0, 0)))
    proj_halves, small_halves, value_halves = [], [], []
    for which in range(2):
        proj_half = exact_dot(local_rows, basis[:, which * half : (which + 1) * half], (1,))
        summed = half_sum(
            jnp.concatenate([proj_half, small[which * small_rows : (which + 1) * small_rows]]),
            ("dp",),
            which,
        )
        proj_halves.append(summed[: proj_half.shape[0]])
        small_halves.append(summed[proj_half.shape[0] :])
        value_halves.append(exact_dot(local_rows, proj_halves[-1], (0,)))
    proj_own = jnp.concatenate(proj_halves, axis=1)
    emb_own, ln_sum = unpack_rows(jnp.concatenate(small_halves), (emb_local, ln_local))
    own_square = jnp.sum(proj_own * proj_own) + jnp.sum(emb_own * emb_own)
    square_total = small_sum(jnp.full((8, 128), own_square), ("own",))[0, 0]
    grad_norm = jnp.sqrt(square_total + jnp.sum(ln_sum * ln_sum) + 1e-06)
    clip_limit = math.sqrt(FF * RANK + emb_count * replicas * owners * width + 4 * width)
    factor = jnp.minimum(1.0, clip_limit / grad_norm)
    count = step_count[0].astype(jnp.float32)
    correct_one = 1.0 - jnp.power(jnp.float32(beta_one), count)
    correct_two = 1.0 - jnp.power(jnp.float32(beta_two), count)
    proj_rows = lax.dynamic_slice_in_dim(proj_own, replica * row_count, row_count, 0)
    fc_grad = factor * proj_rows.reshape(1, 1, row_count, rank_cols)
    fc_m_next, fc_v_next, fc_direction = adam_update(fc_m, fc_v, fc_grad, correct_one, correct_two)
    ln_m_next, ln_v_next, ln_direction = adam_update(
        ln_m, ln_v, factor * ln_sum, correct_one, correct_two
    )
    ln_next = ln_params - learn_rate * ln_direction
    emb_rows = lax.dynamic_index_in_dim(emb_own, replica, 0, keepdims=True).reshape(
        1, 1, emb_count, width
    )
    emb_m_next, emb_v_next, emb_direction = adam_update(
        emb_m, emb_v, factor * emb_rows, correct_one, correct_two
    )
    fc_dir_mine = fc_direction.reshape(row_count, rank_cols).astype(jnp.bfloat16)
    emb_dir_f32 = emb_direction.reshape(emb_count, width)
    emb_dir_high = emb_dir_f32.astype(jnp.bfloat16)
    emb_dir_low = (emb_dir_f32 - emb_dir_high.astype(jnp.float32)).astype(jnp.bfloat16)
    emb_dir_mine = jnp.stack([emb_dir_high, emb_dir_low])
    gathered = butterfly_gather(pack_rows((fc_dir_mine, emb_dir_mine), rank_cols), "dp")
    fc_dir_all, emb_dir_all = jax.vmap(
        lambda packed: unpack_rows(packed, (fc_dir_mine, emb_dir_mine))
    )(gathered)
    fc_dir_all = fc_dir_all.reshape(replicas * row_count, rank_cols)
    emb_dir_all = emb_dir_all[:, 0].astype(jnp.float32) + emb_dir_all[:, 1].astype(jnp.float32)
    weights_next = updated_weights(fc_dir_all, basis, weights_fc[0]).reshape(weights_fc.shape)
    emb_next = (
        emb_weights.astype(jnp.float32) - learn_rate * emb_dir_all.reshape(emb_weights.shape)
    ).astype(jnp.bfloat16)
    subspace = jnp.concatenate(
        [half_sum(value_halves[which], ("own", "dp"), which) for which in range(2)], axis=1
    )
    basis_next = orthogonalize(subspace)
    return (
        fc_m_next,
        fc_v_next,
        fc_direction,
        weights_next,
        basis_next,
        ln_next,
        ln_m_next,
        ln_v_next,
        emb_next,
        emb_m_next,
        emb_v_next,
    )


def solution(mesh):
    in_specs = (
        P("dp", "own", None, None, None),
        P("dp", None, None),
        P("dp", "own", None, None, None),
        P("own", None, None, None),
        P(),
        P("own", "dp", None, None),
        P("own", "dp", None, None),
        P(),
        P(),
        P(),
        P("own", None, None, None),
        P("own", "dp", None, None),
        P("own", "dp", None, None),
        P(),
    )
    out_specs = (
        P("own", "dp", None, None),
        P("own", "dp", None, None),
        P("own", "dp", None, None),
        P("own", None, None, None),
        P(),
        P(),
        P(),
        P(),
        P("own", None, None, None),
        P("own", "dp", None, None),
        P("own", "dp", None, None),
    )
    return jax.shard_map(shards, mesh=mesh, in_specs=in_specs, out_specs=out_specs, check_vma=False)
```

```python
import math

import jax
import jax.numpy as jnp
from jax import lax
from jax.experimental import pallas as pl
from jax.sharding import PartitionSpec as P

FF = 6400
RANK = 256
NS_STEPS = 5


beta_one = 0.9
beta_two = 0.999
adam_eps = 1e-08
learn_rate = 0.02
galore_scale = 0.25


def adam_update(moment_one, moment_two, gradient, correct_one, correct_two):
    moment_one_new = beta_one * moment_one + (1.0 - beta_one) * gradient
    moment_two_new = beta_two * moment_two + (1.0 - beta_two) * gradient * gradient
    direction = moment_one_new / correct_one / (jnp.sqrt(moment_two_new / correct_two) + adam_eps)
    return (moment_one_new, moment_two_new, direction)


def orthogonalize(subspace):
    high = lax.Precision.HIGH
    highest = lax.Precision.HIGHEST
    iterate = subspace * lax.rsqrt(jnp.sum(subspace * subspace) + 1e-06)
    gram_matrix = jnp.dot(iterate.T, iterate, precision=highest)
    identity = jnp.eye(gram_matrix.shape[0], dtype=gram_matrix.dtype)
    product = None
    for sweep_index in range(NS_STEPS):
        step = 1.5 * identity - 0.5 * gram_matrix
        product = step if product is None else jnp.dot(product, step, precision=highest)
        if sweep_index + 1 < NS_STEPS:
            gram_matrix = jnp.dot(
                step, jnp.dot(gram_matrix, step, precision=highest), precision=highest
            )
    return jnp.dot(iterate, product, precision=high)


def row_count_of(piece, cols):
    return -(-piece.size // cols)


def pack_rows(pieces, cols):
    rows = []
    for piece in pieces:
        if piece.ndim == 2 and piece.shape[1] == cols:
            rows.append(piece)
            continue
        flat = piece.reshape(-1)
        flat = jnp.pad(flat, (0, row_count_of(piece, cols) * cols - flat.size))
        rows.append(flat.reshape(-1, cols))
    return jnp.concatenate(rows, axis=0)


def unpack_rows(packed, pieces):
    cols = packed.shape[1]
    out = []
    start = 0
    for piece in pieces:
        count = row_count_of(piece, cols)
        block = packed[start : start + count]
        start += count
        out.append(block.reshape(-1)[: piece.size].reshape(piece.shape))
    return out


def axis_steps(axes):
    steps = []
    for name in axes:
        size = lax.axis_size(name)
        if size & (size - 1):
            return None
        bit = 1
        while bit < size:
            steps.append((name, bit, size))
            bit *= 2
    return steps


def swap_with(values, name, bit, size):
    return lax.ppermute(values, name, [(index, index ^ bit) for index in range(size)])


def run_steps(parts, steps, tied=None, tie_at=0):
    sides = []
    for position, (name, bit, size) in enumerate(steps):
        side = (lax.axis_index(name) // bit) % 2
        half = parts.shape[0] // 2
        keep = lax.dynamic_slice_in_dim(parts, side * half, half, 0)
        send = lax.dynamic_slice_in_dim(parts, (1 - side) * half, half, 0)
        received = swap_with(send, name, bit, size)
        if tied is not None and position == min(tie_at, len(steps) - 1):
            received, tied = lax.optimization_barrier((received, tied))
        parts = keep + received
        sides.append(side)
    for (name, bit, size), side in zip(reversed(steps), reversed(sides)):
        other = swap_with(parts, name, bit, size)
        first = jnp.where(side == 0, parts, other)
        second = jnp.where(side == 0, other, parts)
        parts = jnp.concatenate([first, second], axis=0)
    if tied is not None:
        return parts, tied
    return parts


def half_orders(axes):
    steps = axis_steps(axes)
    if steps is None:
        return None
    low = 1 if len(axes) > 1 else 0
    high = len(steps) - 1
    if high - low < 2:
        return steps, steps
    middle = steps[low:high]
    return steps, steps[:low] + middle[1:] + middle[:1] + steps[high:]


def half_sum(piece, axes, which, tied=None, tie_at=0):
    orders = half_orders(axes)
    if orders is None:
        summed = lax.psum(piece, axes)
        return summed if tied is None else (summed, tied)
    steps = orders[which]
    count = 2 ** len(steps)
    rows = piece.shape[0]
    padded = -(-rows // (8 * count)) * 8 * count
    out = run_steps(jnp.pad(piece, ((0, padded - rows), (0, 0))), steps, tied, tie_at)
    if tied is None:
        return out[:rows]
    return out[0][:rows], out[1]


def butterfly_sum(packed, axes):
    steps = axis_steps(axes)
    if steps is None:
        return lax.psum(packed, axes)
    count = 2 ** len(steps)
    rows, cols = packed.shape
    padded = -(-rows // (8 * count)) * 8 * count
    parts = jnp.pad(packed, ((0, padded - rows), (0, 0)))
    low = 1 if len(axes) > 1 else 0
    high = len(steps) - 1
    if cols % 256 or high - low < 2:
        return run_steps(parts, steps)[:rows]
    middle = steps[low:high]
    other = steps[:low] + middle[1:] + middle[:1] + steps[high:]
    half = cols // 2
    left = run_steps(parts[:, :half], steps)
    right = run_steps(parts[:, half:], other)
    return jnp.concatenate([left, right], axis=1)[:rows]


def small_sum(values, axes):
    steps = axis_steps(axes)
    if steps is None:
        return lax.psum(values, axes)
    for name, bit, size in steps:
        values = values + swap_with(values, name, bit, size)
    return values


def butterfly_gather(piece, name):
    size = lax.axis_size(name)
    if size & (size - 1):
        return lax.all_gather(piece, name, axis=0, tiled=False)
    parts = piece[None]
    bit = size // 2
    levels = 0
    while bit >= 1:
        side = (lax.axis_index(name) // bit) % 2
        other = swap_with(parts, name, bit, size)
        first = jnp.where(side == 0, parts, other)
        second = jnp.where(side == 0, other, parts)
        parts = jnp.concatenate([first, second], axis=0)
        bit //= 2
        levels += 1
    parts = parts.reshape((2,) * levels + piece.shape)
    order = tuple(reversed(range(levels))) + tuple(range(levels, levels + piece.ndim))
    return parts.transpose(order).reshape((size,) + piece.shape)


def update_kernel(direction_ref, basis_ref, weight_ref, out_ref):
    for block in range(direction_ref.shape[0]):
        update = lax.dot_general(
            direction_ref[block],
            basis_ref[...],
            (((1,), (0,)), ((), ())),
            preferred_element_type=jnp.float32,
        )
        out_ref[block] = (
            weight_ref[block].astype(jnp.float32) - learn_rate * galore_scale * update
        ).astype(out_ref.dtype)


def updated_weights(direction_bf16, basis, weights):
    blocks, rows, width = weights.shape
    pieces = split2(basis).T
    depth = pieces.shape[0]
    doubled = jnp.concatenate([direction_bf16] * 2, axis=1).reshape(blocks, rows, depth)
    group = 2 if blocks % 2 == 0 else 1
    return pl.pallas_call(
        update_kernel,
        out_shape=jax.ShapeDtypeStruct(weights.shape, jnp.bfloat16),
        grid=(blocks // group,),
        in_specs=[
            pl.BlockSpec((group, rows, depth), lambda index: (index, 0, 0)),
            pl.BlockSpec((depth, width), lambda index: (0, 0)),
            pl.BlockSpec((group, rows, width), lambda index: (index, 0, 0)),
        ],
        out_specs=pl.BlockSpec((group, rows, width), lambda index: (index, 0, 0)),
    )(doubled, pieces, weights)


def split2(values):
    first = values.astype(jnp.bfloat16)
    second = (values - first.astype(jnp.float32)).astype(jnp.bfloat16)
    return jnp.concatenate([first, second], axis=1)


def exact_dot(lhs_bf16, rhs_f32, contract):
    cols = rhs_f32.shape[1]
    wide = lax.dot_general(
        lhs_bf16,
        split2(rhs_f32),
        ((contract, (0,)), ((), ())),
        preferred_element_type=jnp.float32,
    )
    return wide[:, :cols] + wide[:, cols:]


def shards(
    grads_fc,
    grads_ln,
    grads_emb,
    weights_fc,
    basis,
    fc_m,
    fc_v,
    ln_params,
    ln_m,
    ln_v,
    emb_weights,
    emb_m,
    emb_v,
    step_count,
):
    highest = lax.Precision.HIGHEST
    replicas = lax.axis_size("dp")
    owners = lax.axis_size("own")
    replica = lax.axis_index("dp")
    blocks = grads_fc.shape[2]
    row_count = grads_fc.shape[3]
    width = grads_fc.shape[4]
    rank_cols = basis.shape[1]
    emb_count = grads_emb.shape[3]
    local_rows = grads_fc.reshape(blocks * row_count, width)
    emb_local = grads_emb.reshape(blocks, emb_count, width).astype(jnp.float32)
    ln_local = grads_ln.reshape(4, width).astype(jnp.float32)
    half = rank_cols // 2
    small = pack_rows((emb_local, ln_local), half)
    small_rows = -(-small.shape[0] // 2)
    small = jnp.pad(small, ((0, 2 * small_rows - small.shape[0]), (0, 0)))
    proj_halves, small_halves, value_halves = [], [], []
    for which in range(2):
        proj_half = exact_dot(local_rows, basis[:, which * half : (which + 1) * half], (1,))
        summed = half_sum(
            jnp.concatenate([proj_half, small[which * small_rows : (which + 1) * small_rows]]),
            ("dp",),
            which,
        )
        proj_halves.append(summed[: proj_half.shape[0]])
        small_halves.append(summed[proj_half.shape[0] :])
        value_halves.append(exact_dot(local_rows, proj_halves[-1], (0,)))
    proj_own = jnp.concatenate(proj_halves, axis=1)
    emb_own, ln_sum = unpack_rows(jnp.concatenate(small_halves), (emb_local, ln_local))
    own_square = jnp.sum(proj_own * proj_own) + jnp.sum(emb_own * emb_own)
    square_total = small_sum(jnp.full((8, 128), own_square), ("own",))[0, 0]
    grad_norm = jnp.sqrt(square_total + jnp.sum(ln_sum * ln_sum) + 1e-06)
    clip_limit = math.sqrt(FF * RANK + emb_count * replicas * owners * width + 4 * width)
    factor = jnp.minimum(1.0, clip_limit / grad_norm)
    count = step_count[0].astype(jnp.float32)
    correct_one = 1.0 - jnp.power(jnp.float32(beta_one), count)
    correct_two = 1.0 - jnp.power(jnp.float32(beta_two), count)
    proj_rows = lax.dynamic_slice_in_dim(proj_own, replica * row_count, row_count, 0)
    fc_grad = factor * proj_rows.reshape(1, 1, row_count, rank_cols)
    fc_m_next, fc_v_next, fc_direction = adam_update(fc_m, fc_v, fc_grad, correct_one, correct_two)
    ln_m_next, ln_v_next, ln_direction = adam_update(
        ln_m, ln_v, factor * ln_sum, correct_one, correct_two
    )
    ln_next = ln_params - learn_rate * ln_direction
    emb_rows = lax.dynamic_index_in_dim(emb_own, replica, 0, keepdims=True).reshape(
        1, 1, emb_count, width
    )
    emb_m_next, emb_v_next, emb_direction = adam_update(
        emb_m, emb_v, factor * emb_rows, correct_one, correct_two
    )
    fc_dir_mine = fc_direction.reshape(row_count, rank_cols).astype(jnp.bfloat16)
    emb_dir_f32 = emb_direction.reshape(emb_count, width)
    emb_dir_high = emb_dir_f32.astype(jnp.bfloat16)
    emb_dir_low = (emb_dir_f32 - emb_dir_high.astype(jnp.float32)).astype(jnp.bfloat16)
    emb_dir_mine = jnp.stack([emb_dir_high, emb_dir_low])
    gathered = butterfly_gather(pack_rows((fc_dir_mine, emb_dir_mine), rank_cols), "dp")
    fc_dir_all, emb_dir_all = jax.vmap(
        lambda packed: unpack_rows(packed, (fc_dir_mine, emb_dir_mine))
    )(gathered)
    fc_dir_all = fc_dir_all.reshape(replicas * row_count, rank_cols)
    emb_dir_all = emb_dir_all[:, 0].astype(jnp.float32) + emb_dir_all[:, 1].astype(jnp.float32)
    weights_next = updated_weights(fc_dir_all, basis, weights_fc[0]).reshape(weights_fc.shape)
    emb_next = (
        emb_weights.astype(jnp.float32) - learn_rate * emb_dir_all.reshape(emb_weights.shape)
    ).astype(jnp.bfloat16)
    first_half = half_sum(value_halves[0], ("own", "dp"), 0)
    second_half, weights_next = half_sum(value_halves[1], ("own", "dp"), 1, weights_next, 1)
    subspace = jnp.concatenate([first_half, second_half], axis=1)
    basis_next = orthogonalize(subspace)
    return (
        fc_m_next,
        fc_v_next,
        fc_direction,
        weights_next,
        basis_next,
        ln_next,
        ln_m_next,
        ln_v_next,
        emb_next,
        emb_m_next,
        emb_v_next,
    )


def solution(mesh):
    in_specs = (
        P("dp", "own", None, None, None),
        P("dp", None, None),
        P("dp", "own", None, None, None),
        P("own", None, None, None),
        P(),
        P("own", "dp", None, None),
        P("own", "dp", None, None),
        P(),
        P(),
        P(),
        P("own", None, None, None),
        P("own", "dp", None, None),
        P("own", "dp", None, None),
        P(),
    )
    out_specs = (
        P("own", "dp", None, None),
        P("own", "dp", None, None),
        P("own", "dp", None, None),
        P("own", None, None, None),
        P(),
        P(),
        P(),
        P(),
        P("own", None, None, None),
        P("own", "dp", None, None),
        P("own", "dp", None, None),
    )
    return jax.shard_map(shards, mesh=mesh, in_specs=in_specs, out_specs=out_specs, check_vma=False)
```

```python
import math

import jax
import jax.numpy as jnp
from jax import lax
from jax.experimental import pallas as pl
from jax.sharding import PartitionSpec as P

FF = 6400
RANK = 256
NS_STEPS = 5


beta_one = 0.9
beta_two = 0.999
adam_eps = 1e-08
learn_rate = 0.02
galore_scale = 0.25


def adam_update(moment_one, moment_two, gradient, correct_one, correct_two):
    moment_one_new = beta_one * moment_one + (1.0 - beta_one) * gradient
    moment_two_new = beta_two * moment_two + (1.0 - beta_two) * gradient * gradient
    direction = moment_one_new / correct_one / (jnp.sqrt(moment_two_new / correct_two) + adam_eps)
    return (moment_one_new, moment_two_new, direction)


def orthogonalize(subspace):
    high = lax.Precision.HIGH
    highest = lax.Precision.HIGHEST
    iterate = subspace * lax.rsqrt(jnp.sum(subspace * subspace) + 1e-06)
    gram_matrix = jnp.dot(iterate.T, iterate, precision=highest)
    identity = jnp.eye(gram_matrix.shape[0], dtype=gram_matrix.dtype)
    product = None
    for sweep_index in range(NS_STEPS):
        step = 1.5 * identity - 0.5 * gram_matrix
        product = step if product is None else jnp.dot(product, step, precision=highest)
        if sweep_index + 1 < NS_STEPS:
            gram_matrix = jnp.dot(
                step, jnp.dot(gram_matrix, step, precision=highest), precision=highest
            )
    return jnp.dot(iterate, product, precision=high)


def row_count_of(piece, cols):
    return -(-piece.size // cols)


def pack_rows(pieces, cols):
    rows = []
    for piece in pieces:
        if piece.ndim == 2 and piece.shape[1] == cols:
            rows.append(piece)
            continue
        flat = piece.reshape(-1)
        flat = jnp.pad(flat, (0, row_count_of(piece, cols) * cols - flat.size))
        rows.append(flat.reshape(-1, cols))
    return jnp.concatenate(rows, axis=0)


def unpack_rows(packed, pieces):
    cols = packed.shape[1]
    out = []
    start = 0
    for piece in pieces:
        count = row_count_of(piece, cols)
        block = packed[start : start + count]
        start += count
        out.append(block.reshape(-1)[: piece.size].reshape(piece.shape))
    return out


def axis_steps(axes):
    steps = []
    for name in axes:
        size = lax.axis_size(name)
        if size & (size - 1):
            return None
        bit = 1
        while bit < size:
            steps.append((name, bit, size))
            bit *= 2
    return steps


def swap_with(values, name, bit, size):
    return lax.ppermute(values, name, [(index, index ^ bit) for index in range(size)])


def run_steps(parts, steps, tied=None, tie_at=0):
    sides = []
    for position, (name, bit, size) in enumerate(steps):
        side = (lax.axis_index(name) // bit) % 2
        half = parts.shape[0] // 2
        keep = lax.dynamic_slice_in_dim(parts, side * half, half, 0)
        send = lax.dynamic_slice_in_dim(parts, (1 - side) * half, half, 0)
        received = swap_with(send, name, bit, size)
        if tied is not None and position == min(tie_at, len(steps) - 1):
            received, tied = lax.optimization_barrier((received, tied))
        parts = keep + received
        sides.append(side)
    for (name, bit, size), side in zip(reversed(steps), reversed(sides)):
        other = swap_with(parts, name, bit, size)
        first = jnp.where(side == 0, parts, other)
        second = jnp.where(side == 0, other, parts)
        parts = jnp.concatenate([first, second], axis=0)
    if tied is not None:
        return parts, tied
    return parts


def direct_sum(packed, name):
    size = lax.axis_size(name)
    rows = packed.shape[0]
    block = -(-rows // (8 * size)) * 8
    parts = jnp.pad(packed, ((0, block * size - rows), (0, 0)))
    index = lax.axis_index(name)
    mine = lax.dynamic_slice_in_dim(parts, index * block, block, 0)
    for shift in range(1, size):
        target = (index + shift) % size
        outgoing = lax.dynamic_slice_in_dim(parts, target * block, block, 0)
        mine = mine + lax.ppermute(
            outgoing, name, [(source, (source + shift) % size) for source in range(size)]
        )
    full = jnp.zeros_like(parts)
    full = lax.dynamic_update_slice_in_dim(full, mine, index * block, 0)
    for shift in range(1, size):
        incoming = lax.ppermute(
            mine, name, [(source, (source + shift) % size) for source in range(size)]
        )
        full = lax.dynamic_update_slice_in_dim(full, incoming, ((index - shift) % size) * block, 0)
    return full[:rows]


def half_orders(axes):
    steps = axis_steps(axes)
    if steps is None:
        return None
    low = 1 if len(axes) > 1 else 0
    high = len(steps) - 1
    if high - low < 2:
        return steps, steps
    middle = steps[low:high]
    return steps, steps[:low] + middle[1:] + middle[:1] + steps[high:]


def half_sum(piece, axes, which, tied=None, tie_at=0):
    orders = half_orders(axes)
    if orders is None:
        summed = lax.psum(piece, axes)
        return summed if tied is None else (summed, tied)
    steps = orders[which]
    count = 2 ** len(steps)
    rows = piece.shape[0]
    padded = -(-rows // (8 * count)) * 8 * count
    out = run_steps(jnp.pad(piece, ((0, padded - rows), (0, 0))), steps, tied, tie_at)
    if tied is None:
        return out[:rows]
    return out[0][:rows], out[1]


def butterfly_sum(packed, axes):
    steps = axis_steps(axes)
    if steps is None:
        return lax.psum(packed, axes)
    count = 2 ** len(steps)
    rows, cols = packed.shape
    padded = -(-rows // (8 * count)) * 8 * count
    parts = jnp.pad(packed, ((0, padded - rows), (0, 0)))
    low = 1 if len(axes) > 1 else 0
    high = len(steps) - 1
    if cols % 256 or high - low < 2:
        return run_steps(parts, steps)[:rows]
    middle = steps[low:high]
    other = steps[:low] + middle[1:] + middle[:1] + steps[high:]
    half = cols // 2
    left = run_steps(parts[:, :half], steps)
    right = run_steps(parts[:, half:], other)
    return jnp.concatenate([left, right], axis=1)[:rows]


def small_sum(values, axes):
    steps = axis_steps(axes)
    if steps is None:
        return lax.psum(values, axes)
    for name, bit, size in steps:
        values = values + swap_with(values, name, bit, size)
    return values


def butterfly_gather(piece, name):
    size = lax.axis_size(name)
    if size & (size - 1):
        return lax.all_gather(piece, name, axis=0, tiled=False)
    parts = piece[None]
    bit = size // 2
    levels = 0
    while bit >= 1:
        side = (lax.axis_index(name) // bit) % 2
        other = swap_with(parts, name, bit, size)
        first = jnp.where(side == 0, parts, other)
        second = jnp.where(side == 0, other, parts)
        parts = jnp.concatenate([first, second], axis=0)
        bit //= 2
        levels += 1
    parts = parts.reshape((2,) * levels + piece.shape)
    order = tuple(reversed(range(levels))) + tuple(range(levels, levels + piece.ndim))
    return parts.transpose(order).reshape((size,) + piece.shape)


def update_kernel(direction_ref, basis_ref, weight_ref, out_ref):
    for block in range(direction_ref.shape[0]):
        update = lax.dot_general(
            direction_ref[block],
            basis_ref[...],
            (((1,), (0,)), ((), ())),
            preferred_element_type=jnp.float32,
        )
        out_ref[block] = (
            weight_ref[block].astype(jnp.float32) - learn_rate * galore_scale * update
        ).astype(out_ref.dtype)


def updated_weights(direction_bf16, basis, weights):
    blocks, rows, width = weights.shape
    pieces = split2(basis).T
    depth = pieces.shape[0]
    doubled = jnp.concatenate([direction_bf16] * 2, axis=1).reshape(blocks, rows, depth)
    group = 2 if blocks % 2 == 0 else 1
    return pl.pallas_call(
        update_kernel,
        out_shape=jax.ShapeDtypeStruct(weights.shape, jnp.bfloat16),
        grid=(blocks // group,),
        in_specs=[
            pl.BlockSpec((group, rows, depth), lambda index: (index, 0, 0)),
            pl.BlockSpec((depth, width), lambda index: (0, 0)),
            pl.BlockSpec((group, rows, width), lambda index: (index, 0, 0)),
        ],
        out_specs=pl.BlockSpec((group, rows, width), lambda index: (index, 0, 0)),
    )(doubled, pieces, weights)


def split2(values):
    first = values.astype(jnp.bfloat16)
    second = (values - first.astype(jnp.float32)).astype(jnp.bfloat16)
    return jnp.concatenate([first, second], axis=1)


def exact_dot(lhs_bf16, rhs_f32, contract):
    cols = rhs_f32.shape[1]
    wide = lax.dot_general(
        lhs_bf16,
        split2(rhs_f32),
        ((contract, (0,)), ((), ())),
        preferred_element_type=jnp.float32,
    )
    return wide[:, :cols] + wide[:, cols:]


def shards(
    grads_fc,
    grads_ln,
    grads_emb,
    weights_fc,
    basis,
    fc_m,
    fc_v,
    ln_params,
    ln_m,
    ln_v,
    emb_weights,
    emb_m,
    emb_v,
    step_count,
):
    highest = lax.Precision.HIGHEST
    replicas = lax.axis_size("dp")
    owners = lax.axis_size("own")
    replica = lax.axis_index("dp")
    blocks = grads_fc.shape[2]
    row_count = grads_fc.shape[3]
    width = grads_fc.shape[4]
    rank_cols = basis.shape[1]
    emb_count = grads_emb.shape[3]
    local_rows = grads_fc.reshape(blocks * row_count, width)
    emb_local = grads_emb.reshape(blocks, emb_count, width).astype(jnp.float32)
    ln_local = grads_ln.reshape(4, width).astype(jnp.float32)
    half = rank_cols // 2
    local_proj = exact_dot(local_rows, basis, (1,))
    proj_own, emb_own, ln_sum = unpack_rows(
        direct_sum(pack_rows((local_proj, emb_local, ln_local), rank_cols), "dp"),
        (local_proj, emb_local, ln_local),
    )
    value_halves = [
        exact_dot(local_rows, proj_own[:, which * half : (which + 1) * half], (0,))
        for which in range(2)
    ]
    own_square = jnp.sum(proj_own * proj_own) + jnp.sum(emb_own * emb_own)
    square_total = small_sum(jnp.full((8, 128), own_square), ("own",))[0, 0]
    grad_norm = jnp.sqrt(square_total + jnp.sum(ln_sum * ln_sum) + 1e-06)
    clip_limit = math.sqrt(FF * RANK + emb_count * replicas * owners * width + 4 * width)
    factor = jnp.minimum(1.0, clip_limit / grad_norm)
    count = step_count[0].astype(jnp.float32)
    correct_one = 1.0 - jnp.power(jnp.float32(beta_one), count)
    correct_two = 1.0 - jnp.power(jnp.float32(beta_two), count)
    proj_rows = lax.dynamic_slice_in_dim(proj_own, replica * row_count, row_count, 0)
    fc_grad = factor * proj_rows.reshape(1, 1, row_count, rank_cols)
    fc_m_next, fc_v_next, fc_direction = adam_update(fc_m, fc_v, fc_grad, correct_one, correct_two)
    ln_m_next, ln_v_next, ln_direction = adam_update(
        ln_m, ln_v, factor * ln_sum, correct_one, correct_two
    )
    ln_next = ln_params - learn_rate * ln_direction
    emb_rows = lax.dynamic_index_in_dim(emb_own, replica, 0, keepdims=True).reshape(
        1, 1, emb_count, width
    )
    emb_m_next, emb_v_next, emb_direction = adam_update(
        emb_m, emb_v, factor * emb_rows, correct_one, correct_two
    )
    fc_dir_mine = fc_direction.reshape(row_count, rank_cols).astype(jnp.bfloat16)
    emb_dir_f32 = emb_direction.reshape(emb_count, width)
    emb_dir_high = emb_dir_f32.astype(jnp.bfloat16)
    emb_dir_low = (emb_dir_f32 - emb_dir_high.astype(jnp.float32)).astype(jnp.bfloat16)
    emb_dir_mine = jnp.stack([emb_dir_high, emb_dir_low])
    gathered = butterfly_gather(pack_rows((fc_dir_mine, emb_dir_mine), rank_cols), "dp")
    fc_dir_all, emb_dir_all = jax.vmap(
        lambda packed: unpack_rows(packed, (fc_dir_mine, emb_dir_mine))
    )(gathered)
    fc_dir_all = fc_dir_all.reshape(replicas * row_count, rank_cols)
    emb_dir_all = emb_dir_all[:, 0].astype(jnp.float32) + emb_dir_all[:, 1].astype(jnp.float32)
    weights_next = updated_weights(fc_dir_all, basis, weights_fc[0]).reshape(weights_fc.shape)
    emb_next = (
        emb_weights.astype(jnp.float32) - learn_rate * emb_dir_all.reshape(emb_weights.shape)
    ).astype(jnp.bfloat16)
    first_half = half_sum(value_halves[0], ("own", "dp"), 0)
    second_half, weights_next = half_sum(value_halves[1], ("own", "dp"), 1, weights_next, 1)
    subspace = jnp.concatenate([first_half, second_half], axis=1)
    basis_next = orthogonalize(subspace)
    return (
        fc_m_next,
        fc_v_next,
        fc_direction,
        weights_next,
        basis_next,
        ln_next,
        ln_m_next,
        ln_v_next,
        emb_next,
        emb_m_next,
        emb_v_next,
    )


def solution(mesh):
    in_specs = (
        P("dp", "own", None, None, None),
        P("dp", None, None),
        P("dp", "own", None, None, None),
        P("own", None, None, None),
        P(),
        P("own", "dp", None, None),
        P("own", "dp", None, None),
        P(),
        P(),
        P(),
        P("own", None, None, None),
        P("own", "dp", None, None),
        P("own", "dp", None, None),
        P(),
    )
    out_specs = (
        P("own", "dp", None, None),
        P("own", "dp", None, None),
        P("own", "dp", None, None),
        P("own", None, None, None),
        P(),
        P(),
        P(),
        P(),
        P("own", None, None, None),
        P("own", "dp", None, None),
        P("own", "dp", None, None),
    )
    return jax.shard_map(shards, mesh=mesh, in_specs=in_specs, out_specs=out_specs, check_vma=False)
```

```python
import math

import jax
import jax.numpy as jnp
from jax import lax
from jax.experimental import pallas as pl
from jax.sharding import PartitionSpec as P

FF = 6400
RANK = 256
NS_STEPS = 5


beta_one = 0.9
beta_two = 0.999
adam_eps = 1e-08
learn_rate = 0.02
galore_scale = 0.25


def adam_update(moment_one, moment_two, gradient, correct_one, correct_two):
    moment_one_new = beta_one * moment_one + (1.0 - beta_one) * gradient
    moment_two_new = beta_two * moment_two + (1.0 - beta_two) * gradient * gradient
    direction = moment_one_new / correct_one / (jnp.sqrt(moment_two_new / correct_two) + adam_eps)
    return (moment_one_new, moment_two_new, direction)


def orthogonalize(subspace):
    high = lax.Precision.HIGH
    highest = lax.Precision.HIGHEST
    iterate = subspace * lax.rsqrt(jnp.sum(subspace * subspace) + 1e-06)
    gram_matrix = jnp.dot(iterate.T, iterate, precision=highest)
    identity = jnp.eye(gram_matrix.shape[0], dtype=gram_matrix.dtype)
    product = None
    for sweep_index in range(NS_STEPS):
        step = 1.5 * identity - 0.5 * gram_matrix
        product = step if product is None else jnp.dot(product, step, precision=highest)
        if sweep_index + 1 < NS_STEPS:
            gram_matrix = jnp.dot(
                step, jnp.dot(gram_matrix, step, precision=highest), precision=highest
            )
    return jnp.dot(iterate, product, precision=high)


def row_count_of(piece, cols):
    return -(-piece.size // cols)


def pack_rows(pieces, cols):
    rows = []
    for piece in pieces:
        if piece.ndim == 2 and piece.shape[1] == cols:
            rows.append(piece)
            continue
        flat = piece.reshape(-1)
        flat = jnp.pad(flat, (0, row_count_of(piece, cols) * cols - flat.size))
        rows.append(flat.reshape(-1, cols))
    return jnp.concatenate(rows, axis=0)


def unpack_rows(packed, pieces):
    cols = packed.shape[1]
    out = []
    start = 0
    for piece in pieces:
        count = row_count_of(piece, cols)
        block = packed[start : start + count]
        start += count
        out.append(block.reshape(-1)[: piece.size].reshape(piece.shape))
    return out


def axis_steps(axes):
    steps = []
    for name in axes:
        size = lax.axis_size(name)
        if size & (size - 1):
            return None
        bit = 1
        while bit < size:
            steps.append((name, bit, size))
            bit *= 2
    return steps


def swap_with(values, name, bit, size):
    return lax.ppermute(values, name, [(index, index ^ bit) for index in range(size)])


def place_pair(mine, other, side):
    length = mine.shape[0]
    full = jnp.zeros((2 * length,) + mine.shape[1:], mine.dtype)
    full = lax.dynamic_update_slice_in_dim(full, mine, side * length, 0)
    return lax.dynamic_update_slice_in_dim(full, other, (1 - side) * length, 0)


def run_steps(parts, steps):
    sides = []
    for name, bit, size in steps:
        side = (lax.axis_index(name) // bit) % 2
        half = parts.shape[0] // 2
        keep = lax.dynamic_slice_in_dim(parts, side * half, half, 0)
        send = lax.dynamic_slice_in_dim(parts, (1 - side) * half, half, 0)
        parts = keep + swap_with(send, name, bit, size)
        sides.append(side)
    for (name, bit, size), side in zip(reversed(steps), reversed(sides)):
        other = swap_with(parts, name, bit, size)
        parts = place_pair(parts, other, side)
    return parts


def half_orders(axes):
    steps = axis_steps(axes)
    if steps is None:
        return None
    low = 1 if len(axes) > 1 else 0
    high = len(steps) - 1
    if high - low < 2:
        return steps, steps
    middle = steps[low:high]
    return steps, steps[:low] + middle[1:] + middle[:1] + steps[high:]


def half_sum(piece, axes, which):
    orders = half_orders(axes)
    if orders is None:
        return lax.psum(piece, axes)
    steps = orders[which]
    count = 2 ** len(steps)
    rows = piece.shape[0]
    padded = -(-rows // (8 * count)) * 8 * count
    return run_steps(jnp.pad(piece, ((0, padded - rows), (0, 0))), steps)[:rows]


def butterfly_sum(packed, axes):
    steps = axis_steps(axes)
    if steps is None:
        return lax.psum(packed, axes)
    count = 2 ** len(steps)
    rows, cols = packed.shape
    padded = -(-rows // (8 * count)) * 8 * count
    parts = jnp.pad(packed, ((0, padded - rows), (0, 0)))
    low = 1 if len(axes) > 1 else 0
    high = len(steps) - 1
    if cols % 256 or high - low < 2:
        return run_steps(parts, steps)[:rows]
    middle = steps[low:high]
    other = steps[:low] + middle[1:] + middle[:1] + steps[high:]
    half = cols // 2
    left = run_steps(parts[:, :half], steps)
    right = run_steps(parts[:, half:], other)
    return jnp.concatenate([left, right], axis=1)[:rows]


def small_sum(values, axes):
    steps = axis_steps(axes)
    if steps is None:
        return lax.psum(values, axes)
    for name, bit, size in steps:
        values = values + swap_with(values, name, bit, size)
    return values


def butterfly_gather(piece, name):
    size = lax.axis_size(name)
    if size & (size - 1):
        return lax.all_gather(piece, name, axis=0, tiled=False)
    parts = piece[None]
    bit = size // 2
    levels = 0
    while bit >= 1:
        side = (lax.axis_index(name) // bit) % 2
        other = swap_with(parts, name, bit, size)
        parts = place_pair(parts, other, side)
        bit //= 2
        levels += 1
    parts = parts.reshape((2,) * levels + piece.shape)
    order = tuple(reversed(range(levels))) + tuple(range(levels, levels + piece.ndim))
    return parts.transpose(order).reshape((size,) + piece.shape)


def update_kernel(direction_ref, basis_ref, weight_ref, out_ref):
    for block in range(direction_ref.shape[0]):
        update = lax.dot_general(
            direction_ref[block],
            basis_ref[...],
            (((1,), (0,)), ((), ())),
            preferred_element_type=jnp.float32,
        )
        out_ref[block] = (
            weight_ref[block].astype(jnp.float32) - learn_rate * galore_scale * update
        ).astype(out_ref.dtype)


def updated_weights(direction_bf16, basis, weights):
    blocks, rows, width = weights.shape
    pieces = split2(basis).T
    depth = pieces.shape[0]
    doubled = jnp.concatenate([direction_bf16] * 2, axis=1).reshape(blocks, rows, depth)
    group = 2 if blocks % 2 == 0 else 1
    return pl.pallas_call(
        update_kernel,
        out_shape=jax.ShapeDtypeStruct(weights.shape, jnp.bfloat16),
        grid=(blocks // group,),
        in_specs=[
            pl.BlockSpec((group, rows, depth), lambda index: (index, 0, 0)),
            pl.BlockSpec((depth, width), lambda index: (0, 0)),
            pl.BlockSpec((group, rows, width), lambda index: (index, 0, 0)),
        ],
        out_specs=pl.BlockSpec((group, rows, width), lambda index: (index, 0, 0)),
    )(doubled, pieces, weights)


def split2(values):
    first = values.astype(jnp.bfloat16)
    second = (values - first.astype(jnp.float32)).astype(jnp.bfloat16)
    return jnp.concatenate([first, second], axis=1)


def exact_dot(lhs_bf16, rhs_f32, contract):
    cols = rhs_f32.shape[1]
    wide = lax.dot_general(
        lhs_bf16,
        split2(rhs_f32),
        ((contract, (0,)), ((), ())),
        preferred_element_type=jnp.float32,
    )
    return wide[:, :cols] + wide[:, cols:]


def shards(
    grads_fc,
    grads_ln,
    grads_emb,
    weights_fc,
    basis,
    fc_m,
    fc_v,
    ln_params,
    ln_m,
    ln_v,
    emb_weights,
    emb_m,
    emb_v,
    step_count,
):
    highest = lax.Precision.HIGHEST
    replicas = lax.axis_size("dp")
    owners = lax.axis_size("own")
    replica = lax.axis_index("dp")
    blocks = grads_fc.shape[2]
    row_count = grads_fc.shape[3]
    width = grads_fc.shape[4]
    rank_cols = basis.shape[1]
    emb_count = grads_emb.shape[3]
    local_rows = grads_fc.reshape(blocks * row_count, width)
    emb_local = grads_emb.reshape(blocks, emb_count, width).astype(jnp.float32)
    ln_local = grads_ln.reshape(4, width).astype(jnp.float32)
    half = rank_cols // 2
    small = pack_rows((emb_local, ln_local), half)
    small_rows = -(-small.shape[0] // 2)
    small = jnp.pad(small, ((0, 2 * small_rows - small.shape[0]), (0, 0)))
    proj_halves, small_halves, value_halves = [], [], []
    for which in range(2):
        proj_half = exact_dot(local_rows, basis[:, which * half : (which + 1) * half], (1,))
        summed = half_sum(
            jnp.concatenate([proj_half, small[which * small_rows : (which + 1) * small_rows]]),
            ("dp",),
            which,
        )
        proj_halves.append(summed[: proj_half.shape[0]])
        small_halves.append(summed[proj_half.shape[0] :])
        value_halves.append(exact_dot(local_rows, proj_halves[-1], (0,)))
    proj_own = jnp.concatenate(proj_halves, axis=1)
    emb_own, ln_sum = unpack_rows(jnp.concatenate(small_halves), (emb_local, ln_local))
    own_square = jnp.sum(proj_own * proj_own) + jnp.sum(emb_own * emb_own)
    square_total = small_sum(jnp.full((8, 128), own_square), ("own",))[0, 0]
    grad_norm = jnp.sqrt(square_total + jnp.sum(ln_sum * ln_sum) + 1e-06)
    clip_limit = math.sqrt(FF * RANK + emb_count * replicas * owners * width + 4 * width)
    factor = jnp.minimum(1.0, clip_limit / grad_norm)
    count = step_count[0].astype(jnp.float32)
    correct_one = 1.0 - jnp.power(jnp.float32(beta_one), count)
    correct_two = 1.0 - jnp.power(jnp.float32(beta_two), count)
    proj_rows = lax.dynamic_slice_in_dim(proj_own, replica * row_count, row_count, 0)
    fc_grad = factor * proj_rows.reshape(1, 1, row_count, rank_cols)
    fc_m_next, fc_v_next, fc_direction = adam_update(fc_m, fc_v, fc_grad, correct_one, correct_two)
    ln_m_next, ln_v_next, ln_direction = adam_update(
        ln_m, ln_v, factor * ln_sum, correct_one, correct_two
    )
    ln_next = ln_params - learn_rate * ln_direction
    emb_rows = lax.dynamic_index_in_dim(emb_own, replica, 0, keepdims=True).reshape(
        1, 1, emb_count, width
    )
    emb_m_next, emb_v_next, emb_direction = adam_update(
        emb_m, emb_v, factor * emb_rows, correct_one, correct_two
    )
    fc_dir_mine = fc_direction.reshape(row_count, rank_cols).astype(jnp.bfloat16)
    emb_dir_f32 = emb_direction.reshape(emb_count, width)
    emb_dir_high = emb_dir_f32.astype(jnp.bfloat16)
    emb_dir_low = (emb_dir_f32 - emb_dir_high.astype(jnp.float32)).astype(jnp.bfloat16)
    emb_dir_mine = jnp.stack([emb_dir_high, emb_dir_low])
    gathered = butterfly_gather(pack_rows((fc_dir_mine, emb_dir_mine), rank_cols), "dp")
    fc_dir_all, emb_dir_all = jax.vmap(
        lambda packed: unpack_rows(packed, (fc_dir_mine, emb_dir_mine))
    )(gathered)
    fc_dir_all = fc_dir_all.reshape(replicas * row_count, rank_cols)
    emb_dir_all = emb_dir_all[:, 0].astype(jnp.float32) + emb_dir_all[:, 1].astype(jnp.float32)
    weights_next = updated_weights(fc_dir_all, basis, weights_fc[0]).reshape(weights_fc.shape)
    emb_next = (
        emb_weights.astype(jnp.float32) - learn_rate * emb_dir_all.reshape(emb_weights.shape)
    ).astype(jnp.bfloat16)
    subspace = jnp.concatenate(
        [half_sum(value_halves[which], ("own", "dp"), which) for which in range(2)], axis=1
    )
    basis_next = orthogonalize(subspace)
    return (
        fc_m_next,
        fc_v_next,
        fc_direction,
        weights_next,
        basis_next,
        ln_next,
        ln_m_next,
        ln_v_next,
        emb_next,
        emb_m_next,
        emb_v_next,
    )


def solution(mesh):
    in_specs = (
        P("dp", "own", None, None, None),
        P("dp", None, None),
        P("dp", "own", None, None, None),
        P("own", None, None, None),
        P(),
        P("own", "dp", None, None),
        P("own", "dp", None, None),
        P(),
        P(),
        P(),
        P("own", None, None, None),
        P("own", "dp", None, None),
        P("own", "dp", None, None),
        P(),
    )
    out_specs = (
        P("own", "dp", None, None),
        P("own", "dp", None, None),
        P("own", "dp", None, None),
        P("own", None, None, None),
        P(),
        P(),
        P(),
        P(),
        P("own", None, None, None),
        P("own", "dp", None, None),
        P("own", "dp", None, None),
    )
    return jax.shard_map(shards, mesh=mesh, in_specs=in_specs, out_specs=out_specs, check_vma=False)
```

```python
import math

import jax
import jax.numpy as jnp
from jax import lax
from jax.experimental import pallas as pl
from jax.sharding import PartitionSpec as P

FF = 6400
RANK = 256
NS_STEPS = 5


beta_one = 0.9
beta_two = 0.999
adam_eps = 1e-08
learn_rate = 0.02
galore_scale = 0.25


def adam_update(moment_one, moment_two, gradient, correct_one, correct_two):
    moment_one_new = beta_one * moment_one + (1.0 - beta_one) * gradient
    moment_two_new = beta_two * moment_two + (1.0 - beta_two) * gradient * gradient
    direction = moment_one_new / correct_one / (jnp.sqrt(moment_two_new / correct_two) + adam_eps)
    return (moment_one_new, moment_two_new, direction)


def orthogonalize(subspace):
    high = lax.Precision.HIGH
    highest = lax.Precision.HIGHEST
    iterate = subspace * lax.rsqrt(jnp.sum(subspace * subspace) + 1e-06)
    gram_matrix = jnp.dot(iterate.T, iterate, precision=highest)
    identity = jnp.eye(gram_matrix.shape[0], dtype=gram_matrix.dtype)
    product = None
    for sweep_index in range(NS_STEPS):
        step = 1.5 * identity - 0.5 * gram_matrix
        product = step if product is None else jnp.dot(product, step, precision=highest)
        if sweep_index + 1 < NS_STEPS:
            gram_matrix = jnp.dot(
                step, jnp.dot(gram_matrix, step, precision=highest), precision=highest
            )
    return jnp.dot(iterate, product, precision=high)


def row_count_of(piece, cols):
    return -(-piece.size // cols)


def pack_rows(pieces, cols):
    rows = []
    for piece in pieces:
        if piece.ndim == 2 and piece.shape[1] == cols:
            rows.append(piece)
            continue
        flat = piece.reshape(-1)
        flat = jnp.pad(flat, (0, row_count_of(piece, cols) * cols - flat.size))
        rows.append(flat.reshape(-1, cols))
    return jnp.concatenate(rows, axis=0)


def unpack_rows(packed, pieces):
    cols = packed.shape[1]
    out = []
    start = 0
    for piece in pieces:
        count = row_count_of(piece, cols)
        block = packed[start : start + count]
        start += count
        out.append(block.reshape(-1)[: piece.size].reshape(piece.shape))
    return out


def axis_steps(axes):
    steps = []
    for name in axes:
        size = lax.axis_size(name)
        if size & (size - 1):
            return None
        bit = 1
        while bit < size:
            steps.append((name, bit, size))
            bit *= 2
    return steps


def swap_with(values, name, bit, size):
    return lax.ppermute(values, name, [(index, index ^ bit) for index in range(size)])


def place_pair(mine, other, side):
    length = mine.shape[0]
    full = jnp.zeros((2 * length,) + mine.shape[1:], mine.dtype)
    full = lax.dynamic_update_slice_in_dim(full, mine, side * length, 0)
    return lax.dynamic_update_slice_in_dim(full, other, (1 - side) * length, 0)


def run_steps(parts, steps):
    sides = []
    for name, bit, size in steps:
        side = (lax.axis_index(name) // bit) % 2
        half = parts.shape[0] // 2
        keep = lax.dynamic_slice_in_dim(parts, side * half, half, 0)
        send = lax.dynamic_slice_in_dim(parts, (1 - side) * half, half, 0)
        parts = keep + swap_with(send, name, bit, size)
        sides.append(side)
    for (name, bit, size), side in zip(reversed(steps), reversed(sides)):
        other = swap_with(parts, name, bit, size)
        parts = place_pair(parts, other, side)
    return parts


def half_orders(axes):
    steps = axis_steps(axes)
    if steps is None:
        return None
    low = 1 if len(axes) > 1 else 0
    high = len(steps) - 1
    if high - low < 2:
        return steps, steps
    middle = steps[low:high]
    return steps, steps[:low] + middle[1:] + middle[:1] + steps[high:]


def half_sum(piece, axes, which):
    orders = half_orders(axes)
    if orders is None:
        return lax.psum(piece, axes)
    steps = orders[which]
    count = 2 ** len(steps)
    rows = piece.shape[0]
    padded = -(-rows // count) * count
    return run_steps(jnp.pad(piece, ((0, padded - rows), (0, 0))), steps)[:rows]


def butterfly_sum(packed, axes):
    steps = axis_steps(axes)
    if steps is None:
        return lax.psum(packed, axes)
    count = 2 ** len(steps)
    rows, cols = packed.shape
    padded = -(-rows // (8 * count)) * 8 * count
    parts = jnp.pad(packed, ((0, padded - rows), (0, 0)))
    low = 1 if len(axes) > 1 else 0
    high = len(steps) - 1
    if cols % 256 or high - low < 2:
        return run_steps(parts, steps)[:rows]
    middle = steps[low:high]
    other = steps[:low] + middle[1:] + middle[:1] + steps[high:]
    half = cols // 2
    left = run_steps(parts[:, :half], steps)
    right = run_steps(parts[:, half:], other)
    return jnp.concatenate([left, right], axis=1)[:rows]


def small_sum(values, axes):
    steps = axis_steps(axes)
    if steps is None:
        return lax.psum(values, axes)
    for name, bit, size in steps:
        values = values + swap_with(values, name, bit, size)
    return values


def butterfly_gather(piece, name):
    size = lax.axis_size(name)
    if size & (size - 1):
        return lax.all_gather(piece, name, axis=0, tiled=False)
    parts = piece[None]
    bit = size // 2
    levels = 0
    while bit >= 1:
        side = (lax.axis_index(name) // bit) % 2
        other = swap_with(parts, name, bit, size)
        parts = place_pair(parts, other, side)
        bit //= 2
        levels += 1
    parts = parts.reshape((2,) * levels + piece.shape)
    order = tuple(reversed(range(levels))) + tuple(range(levels, levels + piece.ndim))
    return parts.transpose(order).reshape((size,) + piece.shape)


def update_kernel(direction_ref, basis_ref, weight_ref, out_ref):
    for block in range(direction_ref.shape[0]):
        update = lax.dot_general(
            direction_ref[block],
            basis_ref[...],
            (((1,), (0,)), ((), ())),
            preferred_element_type=jnp.float32,
        )
        out_ref[block] = (
            weight_ref[block].astype(jnp.float32) - learn_rate * galore_scale * update
        ).astype(out_ref.dtype)


def updated_weights(direction_bf16, basis, weights):
    blocks, rows, width = weights.shape
    pieces = split2(basis).T
    depth = pieces.shape[0]
    doubled = jnp.concatenate([direction_bf16] * 2, axis=1).reshape(blocks, rows, depth)
    group = 2 if blocks % 2 == 0 else 1
    return pl.pallas_call(
        update_kernel,
        out_shape=jax.ShapeDtypeStruct(weights.shape, jnp.bfloat16),
        grid=(blocks // group,),
        in_specs=[
            pl.BlockSpec((group, rows, depth), lambda index: (index, 0, 0)),
            pl.BlockSpec((depth, width), lambda index: (0, 0)),
            pl.BlockSpec((group, rows, width), lambda index: (index, 0, 0)),
        ],
        out_specs=pl.BlockSpec((group, rows, width), lambda index: (index, 0, 0)),
    )(doubled, pieces, weights)


def split2(values):
    first = values.astype(jnp.bfloat16)
    second = (values - first.astype(jnp.float32)).astype(jnp.bfloat16)
    return jnp.concatenate([first, second], axis=1)


def exact_dot(lhs_bf16, rhs_f32, contract):
    cols = rhs_f32.shape[1]
    wide = lax.dot_general(
        lhs_bf16,
        split2(rhs_f32),
        ((contract, (0,)), ((), ())),
        preferred_element_type=jnp.float32,
    )
    return wide[:, :cols] + wide[:, cols:]


def shards(
    grads_fc,
    grads_ln,
    grads_emb,
    weights_fc,
    basis,
    fc_m,
    fc_v,
    ln_params,
    ln_m,
    ln_v,
    emb_weights,
    emb_m,
    emb_v,
    step_count,
):
    highest = lax.Precision.HIGHEST
    replicas = lax.axis_size("dp")
    owners = lax.axis_size("own")
    replica = lax.axis_index("dp")
    blocks = grads_fc.shape[2]
    row_count = grads_fc.shape[3]
    width = grads_fc.shape[4]
    rank_cols = basis.shape[1]
    emb_count = grads_emb.shape[3]
    local_rows = grads_fc.reshape(blocks * row_count, width)
    emb_local = grads_emb.reshape(blocks, emb_count, width).astype(jnp.float32)
    ln_local = grads_ln.reshape(4, width).astype(jnp.float32)
    half = rank_cols // 2
    small = pack_rows((emb_local, ln_local), half)
    small_rows = -(-small.shape[0] // 2)
    small = jnp.pad(small, ((0, 2 * small_rows - small.shape[0]), (0, 0)))
    proj_halves, small_halves, value_halves = [], [], []
    for which in range(2):
        proj_half = exact_dot(local_rows, basis[:, which * half : (which + 1) * half], (1,))
        summed = half_sum(
            jnp.concatenate([proj_half, small[which * small_rows : (which + 1) * small_rows]]),
            ("dp",),
            which,
        )
        proj_halves.append(summed[: proj_half.shape[0]])
        small_halves.append(summed[proj_half.shape[0] :])
        value_halves.append(exact_dot(local_rows, proj_halves[-1], (0,)))
    proj_own = jnp.concatenate(proj_halves, axis=1)
    emb_own, ln_sum = unpack_rows(jnp.concatenate(small_halves), (emb_local, ln_local))
    own_square = jnp.sum(proj_own * proj_own) + jnp.sum(emb_own * emb_own)
    square_total = small_sum(jnp.full((8, 128), own_square), ("own",))[0, 0]
    grad_norm = jnp.sqrt(square_total + jnp.sum(ln_sum * ln_sum) + 1e-06)
    clip_limit = math.sqrt(FF * RANK + emb_count * replicas * owners * width + 4 * width)
    factor = jnp.minimum(1.0, clip_limit / grad_norm)
    count = step_count[0].astype(jnp.float32)
    correct_one = 1.0 - jnp.power(jnp.float32(beta_one), count)
    correct_two = 1.0 - jnp.power(jnp.float32(beta_two), count)
    proj_rows = lax.dynamic_slice_in_dim(proj_own, replica * row_count, row_count, 0)
    fc_grad = factor * proj_rows.reshape(1, 1, row_count, rank_cols)
    fc_m_next, fc_v_next, fc_direction = adam_update(fc_m, fc_v, fc_grad, correct_one, correct_two)
    ln_m_next, ln_v_next, ln_direction = adam_update(
        ln_m, ln_v, factor * ln_sum, correct_one, correct_two
    )
    ln_next = ln_params - learn_rate * ln_direction
    emb_rows = lax.dynamic_index_in_dim(emb_own, replica, 0, keepdims=True).reshape(
        1, 1, emb_count, width
    )
    emb_m_next, emb_v_next, emb_direction = adam_update(
        emb_m, emb_v, factor * emb_rows, correct_one, correct_two
    )
    fc_dir_mine = fc_direction.reshape(row_count, rank_cols).astype(jnp.bfloat16)
    emb_dir_f32 = emb_direction.reshape(emb_count, width)
    emb_dir_high = emb_dir_f32.astype(jnp.bfloat16)
    emb_dir_low = (emb_dir_f32 - emb_dir_high.astype(jnp.float32)).astype(jnp.bfloat16)
    emb_dir_mine = jnp.stack([emb_dir_high, emb_dir_low])
    gathered = butterfly_gather(pack_rows((fc_dir_mine, emb_dir_mine), rank_cols), "dp")
    fc_dir_all, emb_dir_all = jax.vmap(
        lambda packed: unpack_rows(packed, (fc_dir_mine, emb_dir_mine))
    )(gathered)
    fc_dir_all = fc_dir_all.reshape(replicas * row_count, rank_cols)
    emb_dir_all = emb_dir_all[:, 0].astype(jnp.float32) + emb_dir_all[:, 1].astype(jnp.float32)
    weights_next = updated_weights(fc_dir_all, basis, weights_fc[0]).reshape(weights_fc.shape)
    emb_next = (
        emb_weights.astype(jnp.float32) - learn_rate * emb_dir_all.reshape(emb_weights.shape)
    ).astype(jnp.bfloat16)
    subspace = jnp.concatenate(
        [half_sum(value_halves[which], ("own", "dp"), which) for which in range(2)], axis=1
    )
    basis_next = orthogonalize(subspace)
    return (
        fc_m_next,
        fc_v_next,
        fc_direction,
        weights_next,
        basis_next,
        ln_next,
        ln_m_next,
        ln_v_next,
        emb_next,
        emb_m_next,
        emb_v_next,
    )


def solution(mesh):
    in_specs = (
        P("dp", "own", None, None, None),
        P("dp", None, None),
        P("dp", "own", None, None, None),
        P("own", None, None, None),
        P(),
        P("own", "dp", None, None),
        P("own", "dp", None, None),
        P(),
        P(),
        P(),
        P("own", None, None, None),
        P("own", "dp", None, None),
        P("own", "dp", None, None),
        P(),
    )
    out_specs = (
        P("own", "dp", None, None),
        P("own", "dp", None, None),
        P("own", "dp", None, None),
        P("own", None, None, None),
        P(),
        P(),
        P(),
        P(),
        P("own", None, None, None),
        P("own", "dp", None, None),
        P("own", "dp", None, None),
    )
    return jax.shard_map(shards, mesh=mesh, in_specs=in_specs, out_specs=out_specs, check_vma=False)
```

```python
import math

import jax
import jax.numpy as jnp
from jax import lax
from jax.experimental import pallas as pl
from jax.sharding import PartitionSpec as P

FF = 6400
RANK = 256
NS_STEPS = 5


beta_one = 0.9
beta_two = 0.999
adam_eps = 1e-08
learn_rate = 0.02
galore_scale = 0.25


def adam_update(moment_one, moment_two, gradient, correct_one, correct_two):
    moment_one_new = beta_one * moment_one + (1.0 - beta_one) * gradient
    moment_two_new = beta_two * moment_two + (1.0 - beta_two) * gradient * gradient
    direction = moment_one_new / correct_one / (jnp.sqrt(moment_two_new / correct_two) + adam_eps)
    return (moment_one_new, moment_two_new, direction)


def orthogonalize(subspace):
    high = lax.Precision.HIGH
    highest = lax.Precision.HIGHEST
    iterate = subspace * lax.rsqrt(jnp.sum(subspace * subspace) + 1e-06)
    gram_matrix = jnp.dot(iterate.T, iterate, precision=highest)
    identity = jnp.eye(gram_matrix.shape[0], dtype=gram_matrix.dtype)
    product = None
    for sweep_index in range(NS_STEPS):
        step = 1.5 * identity - 0.5 * gram_matrix
        product = step if product is None else jnp.dot(product, step, precision=highest)
        if sweep_index + 1 < NS_STEPS:
            gram_matrix = jnp.dot(
                step, jnp.dot(gram_matrix, step, precision=highest), precision=highest
            )
    return jnp.dot(iterate, product, precision=high)


def row_count_of(piece, cols):
    return -(-piece.size // cols)


def pack_rows(pieces, cols):
    rows = []
    for piece in pieces:
        if piece.ndim == 2 and piece.shape[1] == cols:
            rows.append(piece)
            continue
        flat = piece.reshape(-1)
        flat = jnp.pad(flat, (0, row_count_of(piece, cols) * cols - flat.size))
        rows.append(flat.reshape(-1, cols))
    return jnp.concatenate(rows, axis=0)


def unpack_rows(packed, pieces):
    cols = packed.shape[1]
    out = []
    start = 0
    for piece in pieces:
        count = row_count_of(piece, cols)
        block = packed[start : start + count]
        start += count
        out.append(block.reshape(-1)[: piece.size].reshape(piece.shape))
    return out


def axis_steps(axes):
    steps = []
    for name in axes:
        size = lax.axis_size(name)
        if size & (size - 1):
            return None
        bit = 1
        while bit < size:
            steps.append((name, bit, size))
            bit *= 2
    return steps


def swap_with(values, name, bit, size):
    return lax.ppermute(values, name, [(index, index ^ bit) for index in range(size)])


def place_pair(mine, other, side):
    length = mine.shape[0]
    full = jnp.zeros((2 * length,) + mine.shape[1:], mine.dtype)
    full = lax.dynamic_update_slice_in_dim(full, mine, side * length, 0)
    return lax.dynamic_update_slice_in_dim(full, other, (1 - side) * length, 0)


def run_steps(parts, steps):
    sides = []
    for name, bit, size in steps:
        side = (lax.axis_index(name) // bit) % 2
        half = parts.shape[0] // 2
        keep = lax.dynamic_slice_in_dim(parts, side * half, half, 0)
        send = lax.dynamic_slice_in_dim(parts, (1 - side) * half, half, 0)
        parts = keep + swap_with(send, name, bit, size)
        sides.append(side)
    for (name, bit, size), side in zip(reversed(steps), reversed(sides)):
        other = swap_with(parts, name, bit, size)
        parts = place_pair(parts, other, side)
    return parts


def half_orders(axes):
    steps = axis_steps(axes)
    if steps is None:
        return None
    low = 1 if len(axes) > 1 else 0
    high = len(steps) - 1
    if high - low < 2:
        return steps, steps
    middle = steps[low:high]
    return steps, steps[:low] + middle[1:] + middle[:1] + steps[high:]


def half_sum(piece, axes, which):
    orders = half_orders(axes)
    if orders is None:
        return lax.psum(piece, axes)
    steps = orders[which]
    count = 2 ** len(steps)
    rows = piece.shape[0]
    padded = -(-rows // (8 * count)) * 8 * count
    return run_steps(jnp.pad(piece, ((0, padded - rows), (0, 0))), steps)[:rows]


def butterfly_sum(packed, axes):
    steps = axis_steps(axes)
    if steps is None:
        return lax.psum(packed, axes)
    count = 2 ** len(steps)
    rows, cols = packed.shape
    padded = -(-rows // (8 * count)) * 8 * count
    parts = jnp.pad(packed, ((0, padded - rows), (0, 0)))
    low = 1 if len(axes) > 1 else 0
    high = len(steps) - 1
    if cols % 256 or high - low < 2:
        return run_steps(parts, steps)[:rows]
    middle = steps[low:high]
    other = steps[:low] + middle[1:] + middle[:1] + steps[high:]
    half = cols // 2
    left = run_steps(parts[:, :half], steps)
    right = run_steps(parts[:, half:], other)
    return jnp.concatenate([left, right], axis=1)[:rows]


def small_sum(values, axes):
    steps = axis_steps(axes)
    if steps is None:
        return lax.psum(values, axes)
    for name, bit, size in steps:
        values = values + swap_with(values, name, bit, size)
    return values


def butterfly_gather(piece, name):
    size = lax.axis_size(name)
    if size & (size - 1):
        return lax.all_gather(piece, name, axis=0, tiled=False)
    parts = piece[None]
    bit = size // 2
    levels = 0
    while bit >= 1:
        side = (lax.axis_index(name) // bit) % 2
        other = swap_with(parts, name, bit, size)
        parts = place_pair(parts, other, side)
        bit //= 2
        levels += 1
    parts = parts.reshape((2,) * levels + piece.shape)
    order = tuple(reversed(range(levels))) + tuple(range(levels, levels + piece.ndim))
    return parts.transpose(order).reshape((size,) + piece.shape)


def update_kernel(direction_ref, basis_ref, weight_ref, out_ref):
    for block in range(direction_ref.shape[0]):
        update = lax.dot_general(
            direction_ref[block],
            basis_ref[...],
            (((1,), (0,)), ((), ())),
            preferred_element_type=jnp.float32,
        )
        out_ref[block] = (
            weight_ref[block].astype(jnp.float32) - learn_rate * galore_scale * update
        ).astype(out_ref.dtype)


def updated_weights(direction_bf16, basis, weights):
    blocks, rows, width = weights.shape
    pieces = split2(basis).T
    depth = pieces.shape[0]
    doubled = jnp.concatenate([direction_bf16] * 2, axis=1).reshape(blocks, rows, depth)
    group = 4 if blocks % 4 == 0 else 1
    return pl.pallas_call(
        update_kernel,
        out_shape=jax.ShapeDtypeStruct(weights.shape, jnp.bfloat16),
        grid=(blocks // group,),
        in_specs=[
            pl.BlockSpec((group, rows, depth), lambda index: (index, 0, 0)),
            pl.BlockSpec((depth, width), lambda index: (0, 0)),
            pl.BlockSpec((group, rows, width), lambda index: (index, 0, 0)),
        ],
        out_specs=pl.BlockSpec((group, rows, width), lambda index: (index, 0, 0)),
    )(doubled, pieces, weights)


def split2(values):
    first = values.astype(jnp.bfloat16)
    second = (values - first.astype(jnp.float32)).astype(jnp.bfloat16)
    return jnp.concatenate([first, second], axis=1)


def exact_dot(lhs_bf16, rhs_f32, contract):
    cols = rhs_f32.shape[1]
    wide = lax.dot_general(
        lhs_bf16,
        split2(rhs_f32),
        ((contract, (0,)), ((), ())),
        preferred_element_type=jnp.float32,
    )
    return wide[:, :cols] + wide[:, cols:]


def shards(
    grads_fc,
    grads_ln,
    grads_emb,
    weights_fc,
    basis,
    fc_m,
    fc_v,
    ln_params,
    ln_m,
    ln_v,
    emb_weights,
    emb_m,
    emb_v,
    step_count,
):
    highest = lax.Precision.HIGHEST
    replicas = lax.axis_size("dp")
    owners = lax.axis_size("own")
    replica = lax.axis_index("dp")
    blocks = grads_fc.shape[2]
    row_count = grads_fc.shape[3]
    width = grads_fc.shape[4]
    rank_cols = basis.shape[1]
    emb_count = grads_emb.shape[3]
    local_rows = grads_fc.reshape(blocks * row_count, width)
    emb_local = grads_emb.reshape(blocks, emb_count, width).astype(jnp.float32)
    ln_local = grads_ln.reshape(4, width).astype(jnp.float32)
    half = rank_cols // 2
    small = pack_rows((emb_local, ln_local), half)
    small_rows = -(-small.shape[0] // 2)
    small = jnp.pad(small, ((0, 2 * small_rows - small.shape[0]), (0, 0)))
    proj_halves, small_halves, value_halves = [], [], []
    for which in range(2):
        proj_half = exact_dot(local_rows, basis[:, which * half : (which + 1) * half], (1,))
        summed = half_sum(
            jnp.concatenate([proj_half, small[which * small_rows : (which + 1) * small_rows]]),
            ("dp",),
            which,
        )
        proj_halves.append(summed[: proj_half.shape[0]])
        small_halves.append(summed[proj_half.shape[0] :])
        value_halves.append(exact_dot(local_rows, proj_halves[-1], (0,)))
    proj_own = jnp.concatenate(proj_halves, axis=1)
    emb_own, ln_sum = unpack_rows(jnp.concatenate(small_halves), (emb_local, ln_local))
    own_square = jnp.sum(proj_own * proj_own) + jnp.sum(emb_own * emb_own)
    square_total = small_sum(jnp.full((8, 128), own_square), ("own",))[0, 0]
    grad_norm = jnp.sqrt(square_total + jnp.sum(ln_sum * ln_sum) + 1e-06)
    clip_limit = math.sqrt(FF * RANK + emb_count * replicas * owners * width + 4 * width)
    factor = jnp.minimum(1.0, clip_limit / grad_norm)
    count = step_count[0].astype(jnp.float32)
    correct_one = 1.0 - jnp.power(jnp.float32(beta_one), count)
    correct_two = 1.0 - jnp.power(jnp.float32(beta_two), count)
    proj_rows = lax.dynamic_slice_in_dim(proj_own, replica * row_count, row_count, 0)
    fc_grad = factor * proj_rows.reshape(1, 1, row_count, rank_cols)
    fc_m_next, fc_v_next, fc_direction = adam_update(fc_m, fc_v, fc_grad, correct_one, correct_two)
    ln_m_next, ln_v_next, ln_direction = adam_update(
        ln_m, ln_v, factor * ln_sum, correct_one, correct_two
    )
    ln_next = ln_params - learn_rate * ln_direction
    emb_rows = lax.dynamic_index_in_dim(emb_own, replica, 0, keepdims=True).reshape(
        1, 1, emb_count, width
    )
    emb_m_next, emb_v_next, emb_direction = adam_update(
        emb_m, emb_v, factor * emb_rows, correct_one, correct_two
    )
    fc_dir_mine = fc_direction.reshape(row_count, rank_cols).astype(jnp.bfloat16)
    emb_dir_f32 = emb_direction.reshape(emb_count, width)
    emb_dir_high = emb_dir_f32.astype(jnp.bfloat16)
    emb_dir_low = (emb_dir_f32 - emb_dir_high.astype(jnp.float32)).astype(jnp.bfloat16)
    emb_dir_mine = jnp.stack([emb_dir_high, emb_dir_low])
    gathered = butterfly_gather(pack_rows((fc_dir_mine, emb_dir_mine), rank_cols), "dp")
    fc_dir_all, emb_dir_all = jax.vmap(
        lambda packed: unpack_rows(packed, (fc_dir_mine, emb_dir_mine))
    )(gathered)
    fc_dir_all = fc_dir_all.reshape(replicas * row_count, rank_cols)
    emb_dir_all = emb_dir_all[:, 0].astype(jnp.float32) + emb_dir_all[:, 1].astype(jnp.float32)
    weights_next = updated_weights(fc_dir_all, basis, weights_fc[0]).reshape(weights_fc.shape)
    emb_next = (
        emb_weights.astype(jnp.float32) - learn_rate * emb_dir_all.reshape(emb_weights.shape)
    ).astype(jnp.bfloat16)
    subspace = jnp.concatenate(
        [half_sum(value_halves[which], ("own", "dp"), which) for which in range(2)], axis=1
    )
    basis_next = orthogonalize(subspace)
    return (
        fc_m_next,
        fc_v_next,
        fc_direction,
        weights_next,
        basis_next,
        ln_next,
        ln_m_next,
        ln_v_next,
        emb_next,
        emb_m_next,
        emb_v_next,
    )


def solution(mesh):
    in_specs = (
        P("dp", "own", None, None, None),
        P("dp", None, None),
        P("dp", "own", None, None, None),
        P("own", None, None, None),
        P(),
        P("own", "dp", None, None),
        P("own", "dp", None, None),
        P(),
        P(),
        P(),
        P("own", None, None, None),
        P("own", "dp", None, None),
        P("own", "dp", None, None),
        P(),
    )
    out_specs = (
        P("own", "dp", None, None),
        P("own", "dp", None, None),
        P("own", "dp", None, None),
        P("own", None, None, None),
        P(),
        P(),
        P(),
        P(),
        P("own", None, None, None),
        P("own", "dp", None, None),
        P("own", "dp", None, None),
    )
    return jax.shard_map(shards, mesh=mesh, in_specs=in_specs, out_specs=out_specs, check_vma=False)
```

```python
import math

import jax
import jax.numpy as jnp
from jax import lax
from jax.experimental import pallas as pl
from jax.sharding import PartitionSpec as P

FF = 6400
RANK = 256
NS_STEPS = 5


beta_one = 0.9
beta_two = 0.999
adam_eps = 1e-08
learn_rate = 0.02
galore_scale = 0.25


def adam_update(moment_one, moment_two, gradient, correct_one, correct_two):
    moment_one_new = beta_one * moment_one + (1.0 - beta_one) * gradient
    moment_two_new = beta_two * moment_two + (1.0 - beta_two) * gradient * gradient
    direction = moment_one_new / correct_one / (jnp.sqrt(moment_two_new / correct_two) + adam_eps)
    return (moment_one_new, moment_two_new, direction)


def orthogonalize(subspace):
    high = lax.Precision.HIGH
    highest = lax.Precision.HIGHEST
    iterate = subspace * lax.rsqrt(jnp.sum(subspace * subspace) + 1e-06)
    gram_matrix = jnp.dot(iterate.T, iterate, precision=highest)
    identity = jnp.eye(gram_matrix.shape[0], dtype=gram_matrix.dtype)
    product = None
    for sweep_index in range(NS_STEPS):
        step = 1.5 * identity - 0.5 * gram_matrix
        product = step if product is None else jnp.dot(product, step, precision=high)
        if sweep_index + 1 < NS_STEPS:
            gram_matrix = jnp.dot(step, jnp.dot(gram_matrix, step, precision=high), precision=high)
    return jnp.dot(iterate, product, precision=high)


def row_count_of(piece, cols):
    return -(-piece.size // cols)


def pack_rows(pieces, cols):
    rows = []
    for piece in pieces:
        if piece.ndim == 2 and piece.shape[1] == cols:
            rows.append(piece)
            continue
        flat = piece.reshape(-1)
        flat = jnp.pad(flat, (0, row_count_of(piece, cols) * cols - flat.size))
        rows.append(flat.reshape(-1, cols))
    return jnp.concatenate(rows, axis=0)


def unpack_rows(packed, pieces):
    cols = packed.shape[1]
    out = []
    start = 0
    for piece in pieces:
        count = row_count_of(piece, cols)
        block = packed[start : start + count]
        start += count
        out.append(block.reshape(-1)[: piece.size].reshape(piece.shape))
    return out


def axis_steps(axes):
    steps = []
    for name in axes:
        size = lax.axis_size(name)
        if size & (size - 1):
            return None
        bit = 1
        while bit < size:
            steps.append((name, bit, size))
            bit *= 2
    return steps


def swap_with(values, name, bit, size):
    return lax.ppermute(values, name, [(index, index ^ bit) for index in range(size)])


def place_pair(mine, other, side):
    length = mine.shape[0]
    full = jnp.zeros((2 * length,) + mine.shape[1:], mine.dtype)
    full = lax.dynamic_update_slice_in_dim(full, mine, side * length, 0)
    return lax.dynamic_update_slice_in_dim(full, other, (1 - side) * length, 0)


def run_steps(parts, steps):
    sides = []
    for name, bit, size in steps:
        side = (lax.axis_index(name) // bit) % 2
        half = parts.shape[0] // 2
        keep = lax.dynamic_slice_in_dim(parts, side * half, half, 0)
        send = lax.dynamic_slice_in_dim(parts, (1 - side) * half, half, 0)
        parts = keep + swap_with(send, name, bit, size)
        sides.append(side)
    for (name, bit, size), side in zip(reversed(steps), reversed(sides)):
        other = swap_with(parts, name, bit, size)
        parts = place_pair(parts, other, side)
    return parts


def half_orders(axes):
    steps = axis_steps(axes)
    if steps is None:
        return None
    low = 1 if len(axes) > 1 else 0
    high = len(steps) - 1
    if high - low < 2:
        return steps, steps
    middle = steps[low:high]
    return steps, steps[:low] + middle[1:] + middle[:1] + steps[high:]


def half_sum(piece, axes, which):
    orders = half_orders(axes)
    if orders is None:
        return lax.psum(piece, axes)
    steps = orders[which]
    count = 2 ** len(steps)
    rows = piece.shape[0]
    padded = -(-rows // (8 * count)) * 8 * count
    return run_steps(jnp.pad(piece, ((0, padded - rows), (0, 0))), steps)[:rows]


def butterfly_sum(packed, axes):
    steps = axis_steps(axes)
    if steps is None:
        return lax.psum(packed, axes)
    count = 2 ** len(steps)
    rows, cols = packed.shape
    padded = -(-rows // (8 * count)) * 8 * count
    parts = jnp.pad(packed, ((0, padded - rows), (0, 0)))
    low = 1 if len(axes) > 1 else 0
    high = len(steps) - 1
    if cols % 256 or high - low < 2:
        return run_steps(parts, steps)[:rows]
    middle = steps[low:high]
    other = steps[:low] + middle[1:] + middle[:1] + steps[high:]
    half = cols // 2
    left = run_steps(parts[:, :half], steps)
    right = run_steps(parts[:, half:], other)
    return jnp.concatenate([left, right], axis=1)[:rows]


def small_sum(values, axes):
    steps = axis_steps(axes)
    if steps is None:
        return lax.psum(values, axes)
    for name, bit, size in steps:
        values = values + swap_with(values, name, bit, size)
    return values


def butterfly_gather(piece, name):
    size = lax.axis_size(name)
    if size & (size - 1):
        return lax.all_gather(piece, name, axis=0, tiled=False)
    parts = piece[None]
    bit = size // 2
    levels = 0
    while bit >= 1:
        side = (lax.axis_index(name) // bit) % 2
        other = swap_with(parts, name, bit, size)
        parts = place_pair(parts, other, side)
        bit //= 2
        levels += 1
    parts = parts.reshape((2,) * levels + piece.shape)
    order = tuple(reversed(range(levels))) + tuple(range(levels, levels + piece.ndim))
    return parts.transpose(order).reshape((size,) + piece.shape)


def update_kernel(direction_ref, basis_ref, weight_ref, out_ref):
    for block in range(direction_ref.shape[0]):
        update = lax.dot_general(
            direction_ref[block],
            basis_ref[...],
            (((1,), (0,)), ((), ())),
            preferred_element_type=jnp.float32,
        )
        out_ref[block] = (
            weight_ref[block].astype(jnp.float32) - learn_rate * galore_scale * update
        ).astype(out_ref.dtype)


def updated_weights(direction_bf16, basis, weights):
    blocks, rows, width = weights.shape
    pieces = split2(basis).T
    depth = pieces.shape[0]
    doubled = jnp.concatenate([direction_bf16] * 2, axis=1).reshape(blocks, rows, depth)
    group = 4 if blocks % 4 == 0 else 1
    return pl.pallas_call(
        update_kernel,
        out_shape=jax.ShapeDtypeStruct(weights.shape, jnp.bfloat16),
        grid=(blocks // group,),
        in_specs=[
            pl.BlockSpec((group, rows, depth), lambda index: (index, 0, 0)),
            pl.BlockSpec((depth, width), lambda index: (0, 0)),
            pl.BlockSpec((group, rows, width), lambda index: (index, 0, 0)),
        ],
        out_specs=pl.BlockSpec((group, rows, width), lambda index: (index, 0, 0)),
    )(doubled, pieces, weights)


def split2(values):
    first = values.astype(jnp.bfloat16)
    second = (values - first.astype(jnp.float32)).astype(jnp.bfloat16)
    return jnp.concatenate([first, second], axis=1)


def exact_dot(lhs_bf16, rhs_f32, contract):
    cols = rhs_f32.shape[1]
    wide = lax.dot_general(
        lhs_bf16,
        split2(rhs_f32),
        ((contract, (0,)), ((), ())),
        preferred_element_type=jnp.float32,
    )
    return wide[:, :cols] + wide[:, cols:]


def shards(
    grads_fc,
    grads_ln,
    grads_emb,
    weights_fc,
    basis,
    fc_m,
    fc_v,
    ln_params,
    ln_m,
    ln_v,
    emb_weights,
    emb_m,
    emb_v,
    step_count,
):
    highest = lax.Precision.HIGHEST
    replicas = lax.axis_size("dp")
    owners = lax.axis_size("own")
    replica = lax.axis_index("dp")
    blocks = grads_fc.shape[2]
    row_count = grads_fc.shape[3]
    width = grads_fc.shape[4]
    rank_cols = basis.shape[1]
    emb_count = grads_emb.shape[3]
    local_rows = grads_fc.reshape(blocks * row_count, width)
    emb_local = grads_emb.reshape(blocks, emb_count, width).astype(jnp.float32)
    ln_local = grads_ln.reshape(4, width).astype(jnp.float32)
    half = rank_cols // 2
    small = pack_rows((emb_local, ln_local), half)
    small_rows = -(-small.shape[0] // 2)
    small = jnp.pad(small, ((0, 2 * small_rows - small.shape[0]), (0, 0)))
    proj_halves, small_halves, value_halves = [], [], []
    for which in range(2):
        proj_half = exact_dot(local_rows, basis[:, which * half : (which + 1) * half], (1,))
        summed = half_sum(
            jnp.concatenate([proj_half, small[which * small_rows : (which + 1) * small_rows]]),
            ("dp",),
            which,
        )
        proj_halves.append(summed[: proj_half.shape[0]])
        small_halves.append(summed[proj_half.shape[0] :])
        value_halves.append(exact_dot(local_rows, proj_halves[-1], (0,)))
    proj_own = jnp.concatenate(proj_halves, axis=1)
    emb_own, ln_sum = unpack_rows(jnp.concatenate(small_halves), (emb_local, ln_local))
    own_square = jnp.sum(proj_own * proj_own) + jnp.sum(emb_own * emb_own)
    square_total = small_sum(jnp.full((8, 128), own_square), ("own",))[0, 0]
    grad_norm = jnp.sqrt(square_total + jnp.sum(ln_sum * ln_sum) + 1e-06)
    clip_limit = math.sqrt(FF * RANK + emb_count * replicas * owners * width + 4 * width)
    factor = jnp.minimum(1.0, clip_limit / grad_norm)
    count = step_count[0].astype(jnp.float32)
    correct_one = 1.0 - jnp.power(jnp.float32(beta_one), count)
    correct_two = 1.0 - jnp.power(jnp.float32(beta_two), count)
    proj_rows = lax.dynamic_slice_in_dim(proj_own, replica * row_count, row_count, 0)
    fc_grad = factor * proj_rows.reshape(1, 1, row_count, rank_cols)
    fc_m_next, fc_v_next, fc_direction = adam_update(fc_m, fc_v, fc_grad, correct_one, correct_two)
    ln_m_next, ln_v_next, ln_direction = adam_update(
        ln_m, ln_v, factor * ln_sum, correct_one, correct_two
    )
    ln_next = ln_params - learn_rate * ln_direction
    emb_rows = lax.dynamic_index_in_dim(emb_own, replica, 0, keepdims=True).reshape(
        1, 1, emb_count, width
    )
    emb_m_next, emb_v_next, emb_direction = adam_update(
        emb_m, emb_v, factor * emb_rows, correct_one, correct_two
    )
    fc_dir_mine = fc_direction.reshape(row_count, rank_cols).astype(jnp.bfloat16)
    emb_dir_f32 = emb_direction.reshape(emb_count, width)
    emb_dir_high = emb_dir_f32.astype(jnp.bfloat16)
    emb_dir_low = (emb_dir_f32 - emb_dir_high.astype(jnp.float32)).astype(jnp.bfloat16)
    emb_dir_mine = jnp.stack([emb_dir_high, emb_dir_low])
    gathered = butterfly_gather(pack_rows((fc_dir_mine, emb_dir_mine), rank_cols), "dp")
    fc_dir_all, emb_dir_all = jax.vmap(
        lambda packed: unpack_rows(packed, (fc_dir_mine, emb_dir_mine))
    )(gathered)
    fc_dir_all = fc_dir_all.reshape(replicas * row_count, rank_cols)
    emb_dir_all = emb_dir_all[:, 0].astype(jnp.float32) + emb_dir_all[:, 1].astype(jnp.float32)
    weights_next = updated_weights(fc_dir_all, basis, weights_fc[0]).reshape(weights_fc.shape)
    emb_next = (
        emb_weights.astype(jnp.float32) - learn_rate * emb_dir_all.reshape(emb_weights.shape)
    ).astype(jnp.bfloat16)
    subspace = jnp.concatenate(
        [half_sum(value_halves[which], ("own", "dp"), which) for which in range(2)], axis=1
    )
    basis_next = orthogonalize(subspace)
    return (
        fc_m_next,
        fc_v_next,
        fc_direction,
        weights_next,
        basis_next,
        ln_next,
        ln_m_next,
        ln_v_next,
        emb_next,
        emb_m_next,
        emb_v_next,
    )


def solution(mesh):
    in_specs = (
        P("dp", "own", None, None, None),
        P("dp", None, None),
        P("dp", "own", None, None, None),
        P("own", None, None, None),
        P(),
        P("own", "dp", None, None),
        P("own", "dp", None, None),
        P(),
        P(),
        P(),
        P("own", None, None, None),
        P("own", "dp", None, None),
        P("own", "dp", None, None),
        P(),
    )
    out_specs = (
        P("own", "dp", None, None),
        P("own", "dp", None, None),
        P("own", "dp", None, None),
        P("own", None, None, None),
        P(),
        P(),
        P(),
        P(),
        P("own", None, None, None),
        P("own", "dp", None, None),
        P("own", "dp", None, None),
    )
    return jax.shard_map(shards, mesh=mesh, in_specs=in_specs, out_specs=out_specs, check_vma=False)
```

```python
import math

import jax
import jax.numpy as jnp
from jax import lax
from jax.experimental import pallas as pl
from jax.sharding import PartitionSpec as P

FF = 6400
RANK = 256
NS_STEPS = 5


beta_one = 0.9
beta_two = 0.999
adam_eps = 1e-08
learn_rate = 0.02
galore_scale = 0.25


def adam_update(moment_one, moment_two, gradient, correct_one, correct_two):
    moment_one_new = beta_one * moment_one + (1.0 - beta_one) * gradient
    moment_two_new = beta_two * moment_two + (1.0 - beta_two) * gradient * gradient
    direction = moment_one_new / correct_one / (jnp.sqrt(moment_two_new / correct_two) + adam_eps)
    return (moment_one_new, moment_two_new, direction)


def orthogonalize(subspace):
    high = lax.Precision.HIGH
    iterate = subspace * lax.rsqrt(jnp.sum(subspace * subspace) + 1e-06)
    gram_matrix = jnp.dot(iterate.T, iterate, precision=high)
    identity = jnp.eye(gram_matrix.shape[0], dtype=gram_matrix.dtype)
    product = None
    for sweep_index in range(NS_STEPS):
        step = 1.5 * identity - 0.5 * gram_matrix
        product = step if product is None else jnp.dot(product, step, precision=high)
        if sweep_index + 1 < NS_STEPS:
            gram_matrix = jnp.dot(step, jnp.dot(gram_matrix, step, precision=high), precision=high)
    return jnp.dot(iterate, product, precision=high)


def row_count_of(piece, cols):
    return -(-piece.size // cols)


def pack_rows(pieces, cols):
    rows = []
    for piece in pieces:
        if piece.ndim == 2 and piece.shape[1] == cols:
            rows.append(piece)
            continue
        flat = piece.reshape(-1)
        flat = jnp.pad(flat, (0, row_count_of(piece, cols) * cols - flat.size))
        rows.append(flat.reshape(-1, cols))
    return jnp.concatenate(rows, axis=0)


def unpack_rows(packed, pieces):
    cols = packed.shape[1]
    out = []
    start = 0
    for piece in pieces:
        count = row_count_of(piece, cols)
        block = packed[start : start + count]
        start += count
        out.append(block.reshape(-1)[: piece.size].reshape(piece.shape))
    return out


def axis_steps(axes):
    steps = []
    for name in axes:
        size = lax.axis_size(name)
        if size & (size - 1):
            return None
        bit = 1
        while bit < size:
            steps.append((name, bit, size))
            bit *= 2
    return steps


def swap_with(values, name, bit, size):
    return lax.ppermute(values, name, [(index, index ^ bit) for index in range(size)])


def place_pair(mine, other, side):
    length = mine.shape[0]
    full = jnp.zeros((2 * length,) + mine.shape[1:], mine.dtype)
    full = lax.dynamic_update_slice_in_dim(full, mine, side * length, 0)
    return lax.dynamic_update_slice_in_dim(full, other, (1 - side) * length, 0)


def run_steps(parts, steps):
    sides = []
    for name, bit, size in steps:
        side = (lax.axis_index(name) // bit) % 2
        half = parts.shape[0] // 2
        keep = lax.dynamic_slice_in_dim(parts, side * half, half, 0)
        send = lax.dynamic_slice_in_dim(parts, (1 - side) * half, half, 0)
        parts = keep + swap_with(send, name, bit, size)
        sides.append(side)
    for (name, bit, size), side in zip(reversed(steps), reversed(sides)):
        other = swap_with(parts, name, bit, size)
        parts = place_pair(parts, other, side)
    return parts


def half_orders(axes):
    steps = axis_steps(axes)
    if steps is None:
        return None
    low = 1 if len(axes) > 1 else 0
    high = len(steps) - 1
    if high - low < 2:
        return steps, steps
    middle = steps[low:high]
    return steps, steps[:low] + middle[1:] + middle[:1] + steps[high:]


def half_sum(piece, axes, which):
    orders = half_orders(axes)
    if orders is None:
        return lax.psum(piece, axes)
    steps = orders[which]
    count = 2 ** len(steps)
    rows = piece.shape[0]
    padded = -(-rows // (8 * count)) * 8 * count
    return run_steps(jnp.pad(piece, ((0, padded - rows), (0, 0))), steps)[:rows]


def butterfly_sum(packed, axes):
    steps = axis_steps(axes)
    if steps is None:
        return lax.psum(packed, axes)
    count = 2 ** len(steps)
    rows, cols = packed.shape
    padded = -(-rows // (8 * count)) * 8 * count
    parts = jnp.pad(packed, ((0, padded - rows), (0, 0)))
    low = 1 if len(axes) > 1 else 0
    high = len(steps) - 1
    if cols % 256 or high - low < 2:
        return run_steps(parts, steps)[:rows]
    middle = steps[low:high]
    other = steps[:low] + middle[1:] + middle[:1] + steps[high:]
    half = cols // 2
    left = run_steps(parts[:, :half], steps)
    right = run_steps(parts[:, half:], other)
    return jnp.concatenate([left, right], axis=1)[:rows]


def small_sum(values, axes):
    steps = axis_steps(axes)
    if steps is None:
        return lax.psum(values, axes)
    for name, bit, size in steps:
        values = values + swap_with(values, name, bit, size)
    return values


def butterfly_gather(piece, name):
    size = lax.axis_size(name)
    if size & (size - 1):
        return lax.all_gather(piece, name, axis=0, tiled=False)
    parts = piece[None]
    bit = size // 2
    levels = 0
    while bit >= 1:
        side = (lax.axis_index(name) // bit) % 2
        other = swap_with(parts, name, bit, size)
        parts = place_pair(parts, other, side)
        bit //= 2
        levels += 1
    parts = parts.reshape((2,) * levels + piece.shape)
    order = tuple(reversed(range(levels))) + tuple(range(levels, levels + piece.ndim))
    return parts.transpose(order).reshape((size,) + piece.shape)


def update_kernel(direction_ref, basis_ref, weight_ref, out_ref):
    for block in range(direction_ref.shape[0]):
        update = lax.dot_general(
            direction_ref[block],
            basis_ref[...],
            (((1,), (0,)), ((), ())),
            preferred_element_type=jnp.float32,
        )
        out_ref[block] = (
            weight_ref[block].astype(jnp.float32) - learn_rate * galore_scale * update
        ).astype(out_ref.dtype)


def updated_weights(direction_bf16, basis, weights):
    blocks, rows, width = weights.shape
    pieces = split2(basis).T
    depth = pieces.shape[0]
    doubled = jnp.concatenate([direction_bf16] * 2, axis=1).reshape(blocks, rows, depth)
    group = 4 if blocks % 4 == 0 else 1
    return pl.pallas_call(
        update_kernel,
        out_shape=jax.ShapeDtypeStruct(weights.shape, jnp.bfloat16),
        grid=(blocks // group,),
        in_specs=[
            pl.BlockSpec((group, rows, depth), lambda index: (index, 0, 0)),
            pl.BlockSpec((depth, width), lambda index: (0, 0)),
            pl.BlockSpec((group, rows, width), lambda index: (index, 0, 0)),
        ],
        out_specs=pl.BlockSpec((group, rows, width), lambda index: (index, 0, 0)),
    )(doubled, pieces, weights)


def split2(values):
    first = values.astype(jnp.bfloat16)
    second = (values - first.astype(jnp.float32)).astype(jnp.bfloat16)
    return jnp.concatenate([first, second], axis=1)


def exact_dot(lhs_bf16, rhs_f32, contract):
    cols = rhs_f32.shape[1]
    wide = lax.dot_general(
        lhs_bf16,
        split2(rhs_f32),
        ((contract, (0,)), ((), ())),
        preferred_element_type=jnp.float32,
    )
    return wide[:, :cols] + wide[:, cols:]


def shards(
    grads_fc,
    grads_ln,
    grads_emb,
    weights_fc,
    basis,
    fc_m,
    fc_v,
    ln_params,
    ln_m,
    ln_v,
    emb_weights,
    emb_m,
    emb_v,
    step_count,
):
    highest = lax.Precision.HIGHEST
    replicas = lax.axis_size("dp")
    owners = lax.axis_size("own")
    replica = lax.axis_index("dp")
    blocks = grads_fc.shape[2]
    row_count = grads_fc.shape[3]
    width = grads_fc.shape[4]
    rank_cols = basis.shape[1]
    emb_count = grads_emb.shape[3]
    local_rows = grads_fc.reshape(blocks * row_count, width)
    emb_local = grads_emb.reshape(blocks, emb_count, width).astype(jnp.float32)
    ln_local = grads_ln.reshape(4, width).astype(jnp.float32)
    half = rank_cols // 2
    small = pack_rows((emb_local, ln_local), half)
    small_rows = -(-small.shape[0] // 2)
    small = jnp.pad(small, ((0, 2 * small_rows - small.shape[0]), (0, 0)))
    proj_halves, small_halves, value_halves = [], [], []
    for which in range(2):
        proj_half = exact_dot(local_rows, basis[:, which * half : (which + 1) * half], (1,))
        summed = half_sum(
            jnp.concatenate([proj_half, small[which * small_rows : (which + 1) * small_rows]]),
            ("dp",),
            which,
        )
        proj_halves.append(summed[: proj_half.shape[0]])
        small_halves.append(summed[proj_half.shape[0] :])
        value_halves.append(exact_dot(local_rows, proj_halves[-1], (0,)))
    proj_own = jnp.concatenate(proj_halves, axis=1)
    emb_own, ln_sum = unpack_rows(jnp.concatenate(small_halves), (emb_local, ln_local))
    own_square = jnp.sum(proj_own * proj_own) + jnp.sum(emb_own * emb_own)
    square_total = small_sum(jnp.full((8, 128), own_square), ("own",))[0, 0]
    grad_norm = jnp.sqrt(square_total + jnp.sum(ln_sum * ln_sum) + 1e-06)
    clip_limit = math.sqrt(FF * RANK + emb_count * replicas * owners * width + 4 * width)
    factor = jnp.minimum(1.0, clip_limit / grad_norm)
    count = step_count[0].astype(jnp.float32)
    correct_one = 1.0 - jnp.power(jnp.float32(beta_one), count)
    correct_two = 1.0 - jnp.power(jnp.float32(beta_two), count)
    proj_rows = lax.dynamic_slice_in_dim(proj_own, replica * row_count, row_count, 0)
    fc_grad = factor * proj_rows.reshape(1, 1, row_count, rank_cols)
    fc_m_next, fc_v_next, fc_direction = adam_update(fc_m, fc_v, fc_grad, correct_one, correct_two)
    ln_m_next, ln_v_next, ln_direction = adam_update(
        ln_m, ln_v, factor * ln_sum, correct_one, correct_two
    )
    ln_next = ln_params - learn_rate * ln_direction
    emb_rows = lax.dynamic_index_in_dim(emb_own, replica, 0, keepdims=True).reshape(
        1, 1, emb_count, width
    )
    emb_m_next, emb_v_next, emb_direction = adam_update(
        emb_m, emb_v, factor * emb_rows, correct_one, correct_two
    )
    fc_dir_mine = fc_direction.reshape(row_count, rank_cols).astype(jnp.bfloat16)
    emb_dir_f32 = emb_direction.reshape(emb_count, width)
    emb_dir_high = emb_dir_f32.astype(jnp.bfloat16)
    emb_dir_low = (emb_dir_f32 - emb_dir_high.astype(jnp.float32)).astype(jnp.bfloat16)
    emb_dir_mine = jnp.stack([emb_dir_high, emb_dir_low])
    gathered = butterfly_gather(pack_rows((fc_dir_mine, emb_dir_mine), rank_cols), "dp")
    fc_dir_all, emb_dir_all = jax.vmap(
        lambda packed: unpack_rows(packed, (fc_dir_mine, emb_dir_mine))
    )(gathered)
    fc_dir_all = fc_dir_all.reshape(replicas * row_count, rank_cols)
    emb_dir_all = emb_dir_all[:, 0].astype(jnp.float32) + emb_dir_all[:, 1].astype(jnp.float32)
    weights_next = updated_weights(fc_dir_all, basis, weights_fc[0]).reshape(weights_fc.shape)
    emb_next = (
        emb_weights.astype(jnp.float32) - learn_rate * emb_dir_all.reshape(emb_weights.shape)
    ).astype(jnp.bfloat16)
    subspace = jnp.concatenate(
        [half_sum(value_halves[which], ("own", "dp"), which) for which in range(2)], axis=1
    )
    basis_next = orthogonalize(subspace)
    return (
        fc_m_next,
        fc_v_next,
        fc_direction,
        weights_next,
        basis_next,
        ln_next,
        ln_m_next,
        ln_v_next,
        emb_next,
        emb_m_next,
        emb_v_next,
    )


def solution(mesh):
    in_specs = (
        P("dp", "own", None, None, None),
        P("dp", None, None),
        P("dp", "own", None, None, None),
        P("own", None, None, None),
        P(),
        P("own", "dp", None, None),
        P("own", "dp", None, None),
        P(),
        P(),
        P(),
        P("own", None, None, None),
        P("own", "dp", None, None),
        P("own", "dp", None, None),
        P(),
    )
    out_specs = (
        P("own", "dp", None, None),
        P("own", "dp", None, None),
        P("own", "dp", None, None),
        P("own", None, None, None),
        P(),
        P(),
        P(),
        P(),
        P("own", None, None, None),
        P("own", "dp", None, None),
        P("own", "dp", None, None),
    )
    return jax.shard_map(shards, mesh=mesh, in_specs=in_specs, out_specs=out_specs, check_vma=False)
```
